512 devices in a mesh: space: 16 (over x_hi, y, core), seq: 32 (over x_lo, z).
Axes of the slice: x: 4 (x_hi: 2, x_lo: 2; x = x_hi * 2 + x_lo), y: 4, z: 16, core: 2. Of those that a mesh axis runs over, the one named last changes fastest.
Arguments:
- query_feats: bfloat16 [65536, 2048], P(('space', 'seq')), may hold values from -9 to 9
- key_feats: bfloat16 [65536, 2048], P(('space', 'seq')), may hold values from -6 to 6
- value_feats: bfloat16 [65536, 2048], P(('space', 'seq')), may hold values from -6 to 6
- grad_output: bfloat16 [65536, 2048], P(('space', 'seq')), may hold values from -6 to 6
- lengths: int32 [16, 96], replicated, may hold values from 1 to 64, as said below
- members: int32 [1536, 64], P('space'), may hold values from 0 to 4095, as said below
- neighbours: int32 [1536, 5], P('space'), may hold values from 0 to 127, as said below
Outputs:
- attended: bfloat16 [65536, 2048], P(('space', 'seq'))
- grad_queries: bfloat16 [65536, 2048], P(('space', 'seq'))
- grad_keys: bfloat16 [65536, 2048], P(('space', 'seq'))
- grad_values: bfloat16 [65536, 2048], P(('space', 'seq'))
The draws below stay inside these ranges and needn't reach their ends.
Inputs may be any that keep to these rules, and one draw needn't show every extreme that they name: Row g holds the lengths of group g's 96 windows; they sum to 4096, and in every group some window has all 64 slots live. `members`: over a group's windows the live slots (t below the window's length) name each of the group's 4096 voxels exactly once; the other slots name some voxel of the group. `neighbours`: entries index the extended windows of the row's group: below 16 the last 16 windows of the group before, from 16 to 111 its own windows, above that the first 16 windows of the group after. An entry never names the window itself and lies within 16 extended windows of it; group 0 names no window before it and the last group none after it.
All inputs are finite; a program needn't handle non-finite values.
Results may differ from the reference program's by a relative error of at most 0.013.
The reference program's roundings to bfloat16 on the way (of `weights`, `slot_out`, `grad_scores` and `grad_slot_q`) count: a program that leaves them out, or rounds other values in their place, can miss the bound.
Values may be sent and summed in bfloat16 or wider, within the bound.
No kernel may reach another device: no remote copies, remote signals or barrier semaphores. Data moves between devices by JAX's collectives and lax.ppermute only.
A program may use at most 64 MiB of HBM per device.

```python
import jax
import jax.numpy as jnp
from jax import lax

HEADS = 32
HEAD = 64
D = 2048
WIN = 64
NB = 5
GROUPS = 16
VG = 4096
VOXELS = 65536
WG = 96
RIM = 16


def window_layout(key):
    base_key = jax.random.fold_in(key, 11)

    def one_group(group_key):
        cells = WG * (WIN - 1)
        cell_rank = jax.random.permutation(jax.random.fold_in(group_key, 1), cells)
        density = jax.random.randint(jax.random.fold_in(group_key, 2), (WG,), 0, 4)
        full_window = jax.random.randint(jax.random.fold_in(group_key, 3), (), 0, WG)
        density = jnp.where(jnp.arange(WG) == full_window, -1, density)
        row_of_cell = jnp.arange(cells) // (WIN - 1)
        priority = (density[row_of_cell] + 1) * cells + cell_rank
        order = jnp.argsort(priority, stable=True)
        chosen = jnp.zeros((cells,), jnp.int32).at[order].set((jnp.arange(cells) < VG - WG).astype(jnp.int32))
        window_lengths = 1 + chosen.reshape(WG, WIN - 1).sum(axis=1)
        voxel_order = jax.random.permutation(jax.random.fold_in(group_key, 4), VG)
        starts = jnp.cumsum(window_lengths) - window_lengths
        positions = (starts[:, None] + jnp.arange(WIN)[None, :]) % VG
        return (window_lengths.astype(jnp.int32), voxel_order[positions].astype(jnp.int32))
    group_keys = jax.vmap(lambda index: jax.random.fold_in(base_key, index))(jnp.arange(GROUPS))
    return jax.vmap(one_group)(group_keys)


def draw_lengths(key, part):
    window_lengths, member_rows = window_layout(key)
    return window_lengths


def draw_members(key, part):
    window_lengths, member_rows = window_layout(key)
    return member_rows.reshape(GROUPS * WG, WIN)


def draw_neighbours(key, part):
    row_count = GROUPS * WG
    base_key = jax.random.fold_in(key, 51)
    magnitude = jax.random.randint(jax.random.fold_in(base_key, 1), (row_count, NB), 1, RIM + 1)
    direction = jax.random.randint(jax.random.fold_in(base_key, 2), (row_count, NB), 0, 2) * 2 - 1
    row_ids = jnp.arange(row_count)[:, None]
    group_ids = row_ids // WG
    itself = RIM + row_ids % WG
    lowest = jnp.where(group_ids == 0, RIM, 0)
    highest = jnp.where(group_ids == GROUPS - 1, RIM + WG - 1, WG + 2 * RIM - 1)
    picked = jnp.clip(itself + direction * magnitude, lowest, highest)
    picked = jnp.where(picked == itself, jnp.where(direction > 0, itself - magnitude, itself + magnitude), picked)
    return picked.astype(jnp.int32)


def draw_query_feats(key, part):
    values = jax.random.normal(jax.random.fold_in(key, 33), (VOXELS, D), jnp.float32)
    return jnp.clip(values, -6.0, 6.0).astype(jnp.bfloat16)


def draw_key_feats(key, part):
    values = jax.random.normal(jax.random.fold_in(key, 43), (VOXELS, D), jnp.float32)
    return jnp.clip(values, -6.0, 6.0).astype(jnp.bfloat16)


def levels(stream_key, shape, pieces, least, largest):
    factor_of, own = 1.0, jax.random.fold_in(stream_key, 6)
    for position, parts in pieces:
        heights = jnp.exp(jax.random.uniform(jax.random.fold_in(own, position), (parts,), jnp.float32, least / len(pieces), largest / len(pieces)))
        factor_of = factor_of * jnp.repeat(heights, shape[position] // parts).reshape([-1 if axis == position else 1 for axis in range(len(shape))])
    return factor_of


def scatter_about(own_key, dims, deviation, reach, split=(), kind=jnp.bfloat16):
    result = jax.random.normal(own_key, dims, jnp.float32) * deviation
    if len(split) > 0:
        result = levels(own_key, dims, split, -0.22, 0.18) * result
    return jnp.clip(result, min=-reach, max=reach).astype(kind)


def setup_inputs(seed: int = 0) -> dict:
    key_of = jax.random.split(jax.random.key(seed), 8)
    query_feats = draw_query_feats(jax.random.fold_in(key_of[7], 71), 0)
    key_feats = draw_key_feats(jax.random.fold_in(key_of[7], 71), 0)
    value_feats = scatter_about(key_of[2], (VOXELS, D), 1.0, 6.0, ((0, 512),))
    grad_output = scatter_about(key_of[3], (VOXELS, D), 1.0, 6.0, ((0, 512),))
    lengths = draw_lengths(jax.random.fold_in(key_of[7], 71), 0)
    members = draw_members(jax.random.fold_in(key_of[7], 71), 0)
    neighbours = draw_neighbours(jax.random.fold_in(key_of[7], 71), 0)
    return dict(query_feats=query_feats, key_feats=key_feats, value_feats=value_feats, grad_output=grad_output, lengths=lengths, members=members, neighbours=neighbours)


MASKED_SCORE = -1.0e30


def scene_head(query_col, key_col, value_col, grad_col, lengths, members, neighbours):
    groups = lengths.shape[0]
    windows_n = lengths.shape[1]
    border = windows_n // 6
    group_vox = query_col.shape[0] // groups
    member_idx = members.reshape(groups, windows_n, WIN)
    near_idx = neighbours.reshape(groups, windows_n, NB)
    slot_alive = jnp.arange(WIN, dtype=jnp.int32)[None, None, :] < lengths[:, :, None]

    def to_windows(source):
        tables = source.reshape(groups, group_vox, source.shape[-1])
        return jax.vmap(lambda tab, idx: jnp.take(tab, idx, axis=0))(tables, member_idx)

    window_q = to_windows(query_col)
    window_kv = to_windows(jnp.concatenate([key_col, value_col], axis=1))
    window_g = to_windows(grad_col) * slot_alive[..., None].astype(grad_col.dtype)

    pad_kv = jnp.zeros((1, border) + window_kv.shape[2:], window_kv.dtype)
    before_kv = jnp.concatenate([pad_kv, window_kv[:-1, windows_n - border:]], axis=0)
    after_kv = jnp.concatenate([window_kv[1:, :border], pad_kv], axis=0)
    kv_ext = jnp.concatenate([before_kv, window_kv, after_kv], axis=1)
    pad_len = jnp.zeros((1, border), jnp.int32)
    before_len = jnp.concatenate([pad_len, lengths[:-1, windows_n - border:]], axis=0)
    after_len = jnp.concatenate([lengths[1:, :border], pad_len], axis=0)
    length_ext = jnp.concatenate([before_len, lengths, after_len], axis=1)

    own_rows = border + jnp.arange(windows_n, dtype=jnp.int32)
    key_index = jnp.concatenate([jnp.broadcast_to(own_rows[None, :, None], (groups, windows_n, 1)), near_idx], axis=2)
    key_rows = jax.vmap(lambda ext, idx: jnp.take(ext, idx, axis=0))(kv_ext, key_index)
    key_rows = key_rows.reshape(groups, windows_n, (NB + 1) * WIN, 2 * HEAD)
    key_length = jax.vmap(lambda ext, idx: jnp.take(ext, idx, axis=0))(length_ext, key_index)
    key_alive = (jnp.arange(WIN, dtype=jnp.int32)[None, None, None, :] < key_length[..., None]).reshape(groups, windows_n, -1)
    key_part = key_rows[..., :HEAD].astype(jnp.float32)
    value_part = key_rows[..., HEAD:].astype(jnp.float32)
    score_scale = HEAD ** -0.5

    scores = jnp.einsum("gwqd,gwkd->gwqk", window_q.astype(jnp.float32), key_part) * score_scale
    scores = jnp.where(key_alive[:, :, None, :], scores, MASKED_SCORE)
    row_max = jnp.max(scores, axis=-1, keepdims=True)
    exp_scores = jnp.exp(scores - row_max)
    attn_probs = exp_scores / jnp.sum(exp_scores, axis=-1, keepdims=True)
    weights = lax.optimization_barrier(attn_probs.astype(jnp.bfloat16))
    slot_out = jnp.einsum("gwqk,gwkd->gwqd", weights.astype(jnp.float32), value_part)
    slot_out = lax.optimization_barrier(slot_out.astype(jnp.bfloat16))

    row_delta = jnp.sum(window_g.astype(jnp.float32) * slot_out.astype(jnp.float32), axis=-1)
    grad_probs = jnp.einsum("gwqd,gwkd->gwqk", window_g.astype(jnp.float32), value_part)
    grad_scores = (attn_probs * (grad_probs - row_delta[..., None]) * score_scale)
    grad_scores = lax.optimization_barrier(grad_scores.astype(jnp.bfloat16))
    grad_slot_q = jnp.einsum("gwqk,gwkd->gwqd", grad_scores.astype(jnp.float32), key_part).astype(jnp.bfloat16)
    grad_key = jnp.einsum("gwqk,gwqd->gwkd", grad_scores.astype(jnp.float32), window_q.astype(jnp.float32))
    grad_value = jnp.einsum("gwqk,gwqd->gwkd", weights.astype(jnp.float32), window_g.astype(jnp.float32))
    key_terms = jnp.concatenate([grad_key, grad_value], axis=-1).reshape(groups, windows_n, NB + 1, WIN, 2 * HEAD)
    ext_count = windows_n + 2 * border
    grad_ext = jax.vmap(lambda idx, terms: jnp.zeros((ext_count, WIN, 2 * HEAD), jnp.float32).at[idx].add(terms))(key_index, key_terms)

    own_grads = grad_ext[:, border:border + windows_n]
    zero_rim = jnp.zeros((1, border, WIN, 2 * HEAD), jnp.float32)
    from_before = jnp.concatenate([zero_rim, grad_ext[:-1, border + windows_n:]], axis=0)
    from_after = jnp.concatenate([grad_ext[1:, :border], zero_rim], axis=0)
    own_grads = own_grads.at[:, :border].add(from_before)
    own_grads = own_grads.at[:, windows_n - border:].add(from_after)
    slot_kv_grad = own_grads.astype(jnp.bfloat16)

    flat_slots = jnp.where(slot_alive, member_idx, group_vox).reshape(groups, windows_n * WIN)
    slot_of = jax.vmap(lambda slots: jnp.zeros((group_vox,), jnp.int32).at[slots].set(jnp.arange(windows_n * WIN, dtype=jnp.int32), mode="drop"))(flat_slots)

    def to_voxels(slot_vals):
        tables = slot_vals.reshape(groups, windows_n * WIN, slot_vals.shape[-1])
        picked = jax.vmap(lambda tab, idx: jnp.take(tab, idx, axis=0))(tables, slot_of)
        return picked.reshape(groups * group_vox, slot_vals.shape[-1])

    return to_voxels(slot_out), to_voxels(grad_slot_q), to_voxels(slot_kv_grad)


def reference(query_feats, key_feats, value_feats, grad_output, lengths, members, neighbours):
    def one_head(head_idx):
        def head_cols(source):
            return lax.dynamic_slice_in_dim(source, head_idx * HEAD, HEAD, 1)
        return scene_head(head_cols(query_feats), head_cols(key_feats), head_cols(value_feats), head_cols(grad_output), lengths, members, neighbours)

    outputs, grads_q, grads_kv = lax.map(one_head, jnp.arange(HEADS, dtype=jnp.int32))

    def merge_heads(stacked):
        return jnp.transpose(stacked, (1, 0, 2)).reshape(stacked.shape[1], -1)

    return (merge_heads(outputs), merge_heads(grads_q), merge_heads(grads_kv[..., :HEAD]), merge_heads(grads_kv[..., HEAD:]))
```

```python
import jax
import jax.numpy as jnp
from jax import lax
from jax.experimental import pallas as pl
from jax.experimental.pallas import tpu as pltpu
from jax.sharding import PartitionSpec as P

HEAD = 64
WIN = 64


MASKED_SCORE = -1e30


def padded(value, sides, width):
    for axis, dim in sides:
        count, length = (lax.axis_size(axis), value.shape[dim])
        up = [(i, (i + 1) % count) for i in range(count - 1)]
        down = [(j, i) for i, j in up]
        last = lax.slice_in_dim(value, length - width, length, axis=dim)
        first = lax.slice_in_dim(value, 0, width, axis=dim)
        before = lax.ppermute(last, axis, up)
        after = lax.ppermute(first, axis, down)
        value = jnp.concatenate([before, value, after], axis=dim)
    return value


def gather_rows(source, indices):
    return jnp.take(source, indices, axis=0)


def to_windows(query_part, key_part, value_part, members):
    query_win = gather_rows(query_part, members)
    kv_win = gather_rows(jnp.concatenate([key_part, value_part], axis=1), members)
    return (query_win, kv_win)


def border_rows(source, border):
    return jnp.concatenate([source[:border], source[source.shape[0] - border :]], axis=0)


def extend_windows(kv_win, received, border):
    return jnp.concatenate([received[:border], kv_win, received[3 * border :]], axis=0)


def window_keys(block_id, per_block, border, neighbours):
    start_row = block_id * per_block
    own_rows = border + start_row + jnp.arange(per_block, dtype=jnp.int32)
    near_rows = lax.dynamic_slice_in_dim(neighbours, start_row, per_block, 0)
    return jnp.concatenate([own_rows[:, None], near_rows], axis=1)


def block_attention(query_blk, key_index, kv_ext, length_ext, head_count):
    block_n = query_blk.shape[0]
    col_width = query_blk.shape[-1]
    head_size = col_width // head_count
    key_rows = gather_rows(kv_ext, key_index).reshape(block_n, -1, 2 * col_width)
    key_length = gather_rows(length_ext, key_index)
    key_alive = (jnp.arange(WIN, dtype=jnp.int32)[None, None, :] < key_length[:, :, None]).reshape(
        block_n, -1
    )
    query_heads = query_blk.reshape(block_n, WIN, head_count, head_size)
    key_heads = key_rows[:, :, :col_width].reshape(block_n, -1, head_count, head_size)
    value_heads = key_rows[:, :, col_width:].reshape(block_n, -1, head_count, head_size)
    score_scale = head_size ** (-0.5)
    scores = (
        jnp.einsum("wqhd,wkhd->whqk", query_heads, key_heads, preferred_element_type=jnp.float32)
        * score_scale
    )
    scores = jnp.where(key_alive[:, None, None, :], scores, MASKED_SCORE)
    row_max = jnp.max(scores, axis=-1, keepdims=True)
    exp_scores = jnp.exp(scores - row_max)
    attn_probs = exp_scores / jnp.sum(exp_scores, axis=-1, keepdims=True)
    return (attn_probs, query_heads, key_heads, value_heads, score_scale)


def attention_kernel(idx_ref, len_ref, q_ref, k_ref, v_ref, g_ref, out_ref, dq_ref, dk_ref, dv_ref):
    windows_n = q_ref.shape[0]
    nb = idx_ref.shape[0] // windows_n
    keys = nb * WIN
    scale = HEAD ** (-0.5)
    dk_ref[...] = jnp.zeros(dk_ref.shape, dk_ref.dtype)
    dv_ref[...] = jnp.zeros(dv_ref.shape, dv_ref.dtype)
    col = lax.broadcasted_iota(jnp.int32, (1, keys), 1)
    col_block = col // WIN
    col_slot = col % WIN

    def body(w, carry):
        ids = [idx_ref[w * nb + j] for j in range(nb)]
        q = q_ref[w]
        g = g_ref[w]
        k_all = jnp.concatenate([k_ref[i] for i in ids], axis=0)
        v_all = jnp.concatenate([v_ref[i] for i in ids], axis=0)
        limit = jnp.zeros((1, keys), jnp.int32)
        for j in range(nb):
            limit = jnp.where(col_block == j, len_ref[ids[j]], limit)
        alive = col_slot < limit
        nt = (((1,), (1,)), ((), ()))
        tn = (((0,), (0,)), ((), ()))
        scores = lax.dot_general(q, k_all, nt, preferred_element_type=jnp.float32) * scale
        scores = jnp.where(alive, scores, MASKED_SCORE)
        row_max = jnp.max(scores, axis=-1, keepdims=True)
        exp_scores = jnp.exp(scores - row_max)
        probs = exp_scores / jnp.sum(exp_scores, axis=-1, keepdims=True)
        weights = probs.astype(jnp.bfloat16)
        slot_out = jnp.dot(weights, v_all, preferred_element_type=jnp.float32).astype(jnp.bfloat16)
        out_ref[w] = slot_out
        delta = jnp.sum(g.astype(jnp.float32) * slot_out.astype(jnp.float32), axis=-1, keepdims=True)
        grad_probs = lax.dot_general(g, v_all, nt, preferred_element_type=jnp.float32)
        grad_scores = (probs * (grad_probs - delta) * scale).astype(jnp.bfloat16)
        dq_ref[w] = jnp.dot(grad_scores, k_all, preferred_element_type=jnp.float32).astype(jnp.bfloat16)
        grad_k = lax.dot_general(grad_scores, q, tn, preferred_element_type=jnp.float32)
        grad_v = lax.dot_general(weights, g, tn, preferred_element_type=jnp.float32)
        for j in range(nb):
            dk_ref[ids[j]] += grad_k[j * WIN : (j + 1) * WIN]
            dv_ref[ids[j]] += grad_v[j * WIN : (j + 1) * WIN]
        return carry

    lax.fori_loop(0, windows_n, body, 0)


def window_attention(key_index, length_ext, query_win, k_ext, v_ext, grad_win):
    windows_n, _, width = query_win.shape
    ext_n = k_ext.shape[0]
    keys = (key_index.shape[0] // windows_n) * WIN
    flops = 2 * windows_n * WIN * keys * width * 7
    vmem = pl.BlockSpec(memory_space=pltpu.VMEM)
    smem = pl.BlockSpec(memory_space=pltpu.SMEM)
    return pl.pallas_call(
        attention_kernel,
        out_shape=(
            jax.ShapeDtypeStruct(query_win.shape, jnp.bfloat16),
            jax.ShapeDtypeStruct(query_win.shape, jnp.bfloat16),
            jax.ShapeDtypeStruct((ext_n, WIN, width), jnp.float32),
            jax.ShapeDtypeStruct((ext_n, WIN, width), jnp.float32),
        ),
        in_specs=[smem, smem, vmem, vmem, vmem, vmem],
        out_specs=(vmem, vmem, vmem, vmem),
        compiler_params=pltpu.CompilerParams(vmem_limit_bytes=48 * 1024 * 1024),
        cost_estimate=pl.CostEstimate(
            flops=flops, transcendentals=windows_n * WIN * keys, bytes_accessed=8 * 1024 * 1024
        ),
    )(key_index, length_ext, query_win, k_ext, v_ext, grad_win)


def shards(query_feats, key_feats, value_feats, grad_output, lengths, members, neighbours):
    group_idx = lax.axis_index("space")
    groups = lax.axis_size("space")
    windows_n = members.shape[0]
    border = windows_n // 6
    per_block = 8
    block_count = windows_n // per_block
    col_width = query_feats.shape[1] // lax.axis_size("seq")
    head_count = col_width // HEAD
    own_length = lax.dynamic_index_in_dim(lengths, group_idx, 0, keepdims=False)
    before_length = lax.dynamic_index_in_dim(
        lengths, jnp.maximum(group_idx - 1, 0), 0, keepdims=False
    )
    after_length = lax.dynamic_index_in_dim(
        lengths, jnp.minimum(group_idx + 1, groups - 1), 0, keepdims=False
    )
    length_ext = jnp.concatenate(
        [
            jnp.where(group_idx > 0, before_length[windows_n - border :], 0),
            own_length,
            jnp.where(group_idx < groups - 1, after_length[:border], 0),
        ]
    )
    slot_alive = jnp.arange(WIN, dtype=jnp.int32)[None, :] < own_length[:, None]
    query_heads, key_heads, value_heads = (
        lax.all_to_all(query_feats, "seq", split_axis=1, concat_axis=0, tiled=True),
        lax.all_to_all(key_feats, "seq", split_axis=1, concat_axis=0, tiled=True),
        lax.all_to_all(value_feats, "seq", split_axis=1, concat_axis=0, tiled=True),
    )
    voxel_count = query_heads.shape[0]
    flat_slots = jnp.where(slot_alive, members, voxel_count).reshape(-1)
    slot_of = (
        jnp.zeros((voxel_count,), jnp.int32)
        .at[flat_slots]
        .set(jnp.arange(windows_n * WIN, dtype=jnp.int32), mode="drop")
    )

    def to_voxels(slot_vals):
        return gather_rows(slot_vals.reshape(windows_n * WIN, -1), slot_of)

    grad_heads_early = lax.all_to_all(grad_output, "seq", split_axis=1, concat_axis=0, tiled=True)
    query_win, kv_win = to_windows(query_heads, key_heads, value_heads, members)
    received = padded(border_rows(kv_win, border), (("space", 0),), border)
    kv_ext = extend_windows(kv_win, received, border)

    key_index = jnp.concatenate(
        [border + jnp.arange(windows_n, dtype=jnp.int32)[:, None], neighbours], axis=1
    ).reshape(-1)
    k_ext = kv_ext[..., :col_width]
    v_ext = kv_ext[..., col_width:]
    grad_win = gather_rows(grad_heads_early, members) * slot_alive[:, :, None].astype(jnp.bfloat16)
    out_slots, grad_query_blocks, dk_ext, dv_ext = window_attention(
        key_index, length_ext, query_win, k_ext, v_ext, grad_win
    )
    attended = lax.all_to_all(to_voxels(out_slots), "seq", split_axis=0, concat_axis=1, tiled=True)
    grad_ext = jnp.concatenate([dk_ext, dv_ext], axis=-1)
    received_grads = padded(
        border_rows(grad_ext, border).astype(jnp.bfloat16), (("space", 0),), border
    ).astype(jnp.float32)
    own_grads = grad_ext[border : border + windows_n]
    own_grads = own_grads.at[:border].add(received_grads[:border])
    own_grads = own_grads.at[windows_n - border :].add(received_grads[3 * border :])
    kv_grads = to_voxels(own_grads.astype(jnp.bfloat16))
    grad_q_vox = to_voxels(grad_query_blocks.reshape(windows_n, WIN, col_width))
    grad_queries, grad_keys, grad_values = (
        lax.all_to_all(grad_q_vox, "seq", split_axis=0, concat_axis=1, tiled=True),
        lax.all_to_all(kv_grads[:, :col_width], "seq", split_axis=0, concat_axis=1, tiled=True),
        lax.all_to_all(kv_grads[:, col_width:], "seq", split_axis=0, concat_axis=1, tiled=True),
    )
    return (attended, grad_queries, grad_keys, grad_values)


def solution(mesh):
    in_specs = (
        P(("space", "seq"), None),
        P(("space", "seq"), None),
        P(("space", "seq"), None),
        P(("space", "seq"), None),
        P(),
        P("space", None),
        P("space", None),
    )
    out_specs = (
        P(("space", "seq"), None),
        P(("space", "seq"), None),
        P(("space", "seq"), None),
        P(("space", "seq"), None),
    )
    return jax.shard_map(shards, mesh=mesh, in_specs=in_specs, out_specs=out_specs, check_vma=False)
```

```python
import jax
import jax.numpy as jnp
from jax import lax
from jax.experimental import pallas as pl
from jax.experimental.pallas import tpu as pltpu
from jax.sharding import PartitionSpec as P

HEAD = 64
WIN = 64


MASKED_SCORE = -1e30


def padded(value, sides, width):
    for axis, dim in sides:
        count, length = (lax.axis_size(axis), value.shape[dim])
        up = [(i, (i + 1) % count) for i in range(count - 1)]
        down = [(j, i) for i, j in up]
        last = lax.slice_in_dim(value, length - width, length, axis=dim)
        first = lax.slice_in_dim(value, 0, width, axis=dim)
        before = lax.ppermute(last, axis, up)
        after = lax.ppermute(first, axis, down)
        value = jnp.concatenate([before, value, after], axis=dim)
    return value


def gather_rows(source, indices):
    return jnp.take(source, indices, axis=0)


def to_windows(query_part, key_part, value_part, members):
    query_win = gather_rows(query_part, members)
    kv_win = gather_rows(jnp.concatenate([key_part, value_part], axis=1), members)
    return (query_win, kv_win)


def border_rows(source, border):
    return jnp.concatenate([source[:border], source[source.shape[0] - border :]], axis=0)


def extend_windows(kv_win, received, border):
    return jnp.concatenate([received[:border], kv_win, received[3 * border :]], axis=0)


def window_keys(block_id, per_block, border, neighbours):
    start_row = block_id * per_block
    own_rows = border + start_row + jnp.arange(per_block, dtype=jnp.int32)
    near_rows = lax.dynamic_slice_in_dim(neighbours, start_row, per_block, 0)
    return jnp.concatenate([own_rows[:, None], near_rows], axis=1)


def block_attention(query_blk, key_index, kv_ext, length_ext, head_count):
    block_n = query_blk.shape[0]
    col_width = query_blk.shape[-1]
    head_size = col_width // head_count
    key_rows = gather_rows(kv_ext, key_index).reshape(block_n, -1, 2 * col_width)
    key_length = gather_rows(length_ext, key_index)
    key_alive = (jnp.arange(WIN, dtype=jnp.int32)[None, None, :] < key_length[:, :, None]).reshape(
        block_n, -1
    )
    query_heads = query_blk.reshape(block_n, WIN, head_count, head_size)
    key_heads = key_rows[:, :, :col_width].reshape(block_n, -1, head_count, head_size)
    value_heads = key_rows[:, :, col_width:].reshape(block_n, -1, head_count, head_size)
    score_scale = head_size ** (-0.5)
    scores = (
        jnp.einsum("wqhd,wkhd->whqk", query_heads, key_heads, preferred_element_type=jnp.float32)
        * score_scale
    )
    scores = jnp.where(key_alive[:, None, None, :], scores, MASKED_SCORE)
    row_max = jnp.max(scores, axis=-1, keepdims=True)
    exp_scores = jnp.exp(scores - row_max)
    attn_probs = exp_scores / jnp.sum(exp_scores, axis=-1, keepdims=True)
    return (attn_probs, query_heads, key_heads, value_heads, score_scale)


def attention_kernel(idx_ref, len_ref, q_ref, k_ref, v_ref, g_ref, out_ref, dq_ref, dk_ref, dv_ref):
    windows_n = q_ref.shape[0]
    nb = idx_ref.shape[0] // windows_n
    keys = nb * WIN
    scale = HEAD ** (-0.5)
    dk_ref[...] = jnp.zeros(dk_ref.shape, dk_ref.dtype)
    dv_ref[...] = jnp.zeros(dv_ref.shape, dv_ref.dtype)
    col = lax.broadcasted_iota(jnp.int32, (1, keys), 1)
    col_block = col // WIN
    col_slot = col % WIN

    def body(w, carry):
        ids = [idx_ref[w * nb + j] for j in range(nb)]
        q = q_ref[w]
        g = g_ref[w]
        k_all = jnp.concatenate([k_ref[i] for i in ids], axis=0)
        v_all = jnp.concatenate([v_ref[i] for i in ids], axis=0)
        limit = jnp.zeros((1, keys), jnp.int32)
        for j in range(nb):
            limit = jnp.where(col_block == j, len_ref[ids[j]], limit)
        alive = col_slot < limit
        nt = (((1,), (1,)), ((), ()))
        tn = (((0,), (0,)), ((), ()))
        scores = lax.dot_general(q, k_all, nt, preferred_element_type=jnp.float32) * scale
        scores = jnp.where(alive, scores, MASKED_SCORE)
        row_max = jnp.max(scores, axis=-1, keepdims=True)
        exp_scores = jnp.exp(scores - row_max)
        probs = exp_scores / jnp.sum(exp_scores, axis=-1, keepdims=True)
        weights = probs.astype(jnp.bfloat16)
        slot_out = jnp.dot(weights, v_all, preferred_element_type=jnp.float32).astype(jnp.bfloat16)
        out_ref[w] = slot_out
        delta = jnp.sum(g.astype(jnp.float32) * slot_out.astype(jnp.float32), axis=-1, keepdims=True)
        grad_probs = lax.dot_general(g, v_all, nt, preferred_element_type=jnp.float32)
        grad_scores = (probs * (grad_probs - delta) * scale).astype(jnp.bfloat16)
        dq_ref[w] = jnp.dot(grad_scores, k_all, preferred_element_type=jnp.float32).astype(jnp.bfloat16)
        grad_k = lax.dot_general(grad_scores, q, tn, preferred_element_type=jnp.float32)
        grad_v = lax.dot_general(weights, g, tn, preferred_element_type=jnp.float32)
        for j in range(nb):
            dk_ref[ids[j]] += grad_k[j * WIN : (j + 1) * WIN]
            dv_ref[ids[j]] += grad_v[j * WIN : (j + 1) * WIN]
        return carry

    lax.fori_loop(0, windows_n, body, 0)


def window_attention(key_index, length_ext, query_win, k_ext, v_ext, grad_win):
    windows_n, _, width = query_win.shape
    ext_n = k_ext.shape[0]
    keys = (key_index.shape[0] // windows_n) * WIN
    flops = 2 * windows_n * WIN * keys * width * 7
    vmem = pl.BlockSpec(memory_space=pltpu.VMEM)
    smem = pl.BlockSpec(memory_space=pltpu.SMEM)
    return pl.pallas_call(
        attention_kernel,
        out_shape=(
            jax.ShapeDtypeStruct(query_win.shape, jnp.bfloat16),
            jax.ShapeDtypeStruct(query_win.shape, jnp.bfloat16),
            jax.ShapeDtypeStruct((ext_n, WIN, width), jnp.float32),
            jax.ShapeDtypeStruct((ext_n, WIN, width), jnp.float32),
        ),
        in_specs=[smem, smem, vmem, vmem, vmem, vmem],
        out_specs=(vmem, vmem, vmem, vmem),
        compiler_params=pltpu.CompilerParams(vmem_limit_bytes=48 * 1024 * 1024),
        cost_estimate=pl.CostEstimate(
            flops=flops, transcendentals=windows_n * WIN * keys, bytes_accessed=8 * 1024 * 1024
        ),
    )(key_index, length_ext, query_win, k_ext, v_ext, grad_win)


def shards(query_feats, key_feats, value_feats, grad_output, lengths, members, neighbours):
    group_idx = lax.axis_index("space")
    groups = lax.axis_size("space")
    windows_n = members.shape[0]
    border = windows_n // 6
    per_block = 8
    block_count = windows_n // per_block
    col_width = query_feats.shape[1] // lax.axis_size("seq")
    head_count = col_width // HEAD
    own_length = lax.dynamic_index_in_dim(lengths, group_idx, 0, keepdims=False)
    before_length = lax.dynamic_index_in_dim(
        lengths, jnp.maximum(group_idx - 1, 0), 0, keepdims=False
    )
    after_length = lax.dynamic_index_in_dim(
        lengths, jnp.minimum(group_idx + 1, groups - 1), 0, keepdims=False
    )
    length_ext = jnp.concatenate(
        [
            jnp.where(group_idx > 0, before_length[windows_n - border :], 0),
            own_length,
            jnp.where(group_idx < groups - 1, after_length[:border], 0),
        ]
    )
    slot_alive = jnp.arange(WIN, dtype=jnp.int32)[None, :] < own_length[:, None]
    rows = query_feats.shape[0]
    seq_n = lax.axis_size("seq")
    stacked = jnp.stack([query_feats, key_feats, value_feats, grad_output], axis=1)
    stacked = stacked.reshape(rows, 4, seq_n, col_width)
    heads_all = lax.all_to_all(stacked, "seq", split_axis=2, concat_axis=0, tiled=True)
    voxel_count = heads_all.shape[0]
    table = heads_all.reshape(voxel_count, 4 * col_width)
    flat_slots = jnp.where(slot_alive, members, voxel_count).reshape(-1)
    slot_of = (
        jnp.zeros((voxel_count,), jnp.int32)
        .at[flat_slots]
        .set(jnp.arange(windows_n * WIN, dtype=jnp.int32), mode="drop")
    )

    def to_voxels(slot_vals):
        return gather_rows(slot_vals.reshape(windows_n * WIN, -1), slot_of)

    win_all = gather_rows(table, members)
    query_win = win_all[..., :col_width]
    kv_win = win_all[..., col_width : 3 * col_width]
    grad_win = win_all[..., 3 * col_width :] * slot_alive[:, :, None].astype(jnp.bfloat16)
    received = padded(border_rows(kv_win, border), (("space", 0),), border)
    kv_ext = extend_windows(kv_win, received, border)

    key_index = jnp.concatenate(
        [border + jnp.arange(windows_n, dtype=jnp.int32)[:, None], neighbours], axis=1
    ).reshape(-1)
    k_ext = kv_ext[..., :col_width]
    v_ext = kv_ext[..., col_width:]
    out_slots, grad_query_blocks, dk_ext, dv_ext = window_attention(
        key_index, length_ext, query_win, k_ext, v_ext, grad_win
    )
    grad_ext = jnp.concatenate([dk_ext, dv_ext], axis=-1)
    received_grads = padded(
        border_rows(grad_ext, border).astype(jnp.bfloat16), (("space", 0),), border
    ).astype(jnp.float32)
    own_grads = grad_ext[border : border + windows_n]
    own_grads = own_grads.at[:border].add(received_grads[:border])
    own_grads = own_grads.at[windows_n - border :].add(received_grads[3 * border :])
    slot_vals = jnp.concatenate(
        [out_slots, grad_query_blocks, own_grads.astype(jnp.bfloat16)], axis=-1
    )
    vox = to_voxels(slot_vals).reshape(voxel_count, 4, 1, col_width)
    back = lax.all_to_all(vox, "seq", split_axis=0, concat_axis=2, tiled=True)
    back = back.reshape(rows, 4, seq_n * col_width)
    return (back[:, 0], back[:, 1], back[:, 2], back[:, 3])


def solution(mesh):
    in_specs = (
        P(("space", "seq"), None),
        P(("space", "seq"), None),
        P(("space", "seq"), None),
        P(("space", "seq"), None),
        P(),
        P("space", None),
        P("space", None),
    )
    out_specs = (
        P(("space", "seq"), None),
        P(("space", "seq"), None),
        P(("space", "seq"), None),
        P(("space", "seq"), None),
    )
    return jax.shard_map(shards, mesh=mesh, in_specs=in_specs, out_specs=out_specs, check_vma=False)
```

```python
import jax
import jax.numpy as jnp
from jax import lax
from jax.experimental import pallas as pl
from jax.experimental.pallas import tpu as pltpu
from jax.sharding import PartitionSpec as P

HEAD = 64
WIN = 64


MASKED_SCORE = -1e30


def padded(value, sides, width):
    for axis, dim in sides:
        count, length = (lax.axis_size(axis), value.shape[dim])
        up = [(i, (i + 1) % count) for i in range(count - 1)]
        down = [(j, i) for i, j in up]
        last = lax.slice_in_dim(value, length - width, length, axis=dim)
        first = lax.slice_in_dim(value, 0, width, axis=dim)
        before = lax.ppermute(last, axis, up)
        after = lax.ppermute(first, axis, down)
        value = jnp.concatenate([before, value, after], axis=dim)
    return value


def gather_rows(source, indices):
    return jnp.take(source, indices, axis=0)


def to_windows(query_part, key_part, value_part, members):
    query_win = gather_rows(query_part, members)
    kv_win = gather_rows(jnp.concatenate([key_part, value_part], axis=1), members)
    return (query_win, kv_win)


def border_rows(source, border):
    return jnp.concatenate([source[:border], source[source.shape[0] - border :]], axis=0)


def extend_windows(kv_win, received, border):
    return jnp.concatenate([received[:border], kv_win, received[3 * border :]], axis=0)


def window_keys(block_id, per_block, border, neighbours):
    start_row = block_id * per_block
    own_rows = border + start_row + jnp.arange(per_block, dtype=jnp.int32)
    near_rows = lax.dynamic_slice_in_dim(neighbours, start_row, per_block, 0)
    return jnp.concatenate([own_rows[:, None], near_rows], axis=1)


def block_attention(query_blk, key_index, kv_ext, length_ext, head_count):
    block_n = query_blk.shape[0]
    col_width = query_blk.shape[-1]
    head_size = col_width // head_count
    key_rows = gather_rows(kv_ext, key_index).reshape(block_n, -1, 2 * col_width)
    key_length = gather_rows(length_ext, key_index)
    key_alive = (jnp.arange(WIN, dtype=jnp.int32)[None, None, :] < key_length[:, :, None]).reshape(
        block_n, -1
    )
    query_heads = query_blk.reshape(block_n, WIN, head_count, head_size)
    key_heads = key_rows[:, :, :col_width].reshape(block_n, -1, head_count, head_size)
    value_heads = key_rows[:, :, col_width:].reshape(block_n, -1, head_count, head_size)
    score_scale = head_size ** (-0.5)
    scores = (
        jnp.einsum("wqhd,wkhd->whqk", query_heads, key_heads, preferred_element_type=jnp.float32)
        * score_scale
    )
    scores = jnp.where(key_alive[:, None, None, :], scores, MASKED_SCORE)
    row_max = jnp.max(scores, axis=-1, keepdims=True)
    exp_scores = jnp.exp(scores - row_max)
    attn_probs = exp_scores / jnp.sum(exp_scores, axis=-1, keepdims=True)
    return (attn_probs, query_heads, key_heads, value_heads, score_scale)


def attention_kernel(idx_ref, len_ref, q_ref, k_ref, v_ref, g_ref, out_ref, dq_ref, dk_ref, dv_ref):
    windows_n = q_ref.shape[0]
    nb = idx_ref.shape[0] // windows_n
    keys = nb * WIN
    scale = HEAD ** (-0.5)
    dk_ref[...] = jnp.zeros(dk_ref.shape, dk_ref.dtype)
    dv_ref[...] = jnp.zeros(dv_ref.shape, dv_ref.dtype)
    col = lax.broadcasted_iota(jnp.int32, (1, keys), 1)
    col_block = col // WIN
    col_slot = col % WIN

    def body(w, carry):
        ids = [idx_ref[w * nb + j] for j in range(nb)]
        q = q_ref[w]
        g = g_ref[w]
        k_all = jnp.concatenate([k_ref[i] for i in ids], axis=0)
        v_all = jnp.concatenate([v_ref[i] for i in ids], axis=0)
        limit = jnp.zeros((1, keys), jnp.int32)
        for j in range(nb):
            limit = jnp.where(col_block == j, len_ref[ids[j]], limit)
        alive = col_slot < limit
        nt = (((1,), (1,)), ((), ()))
        tn = (((0,), (0,)), ((), ()))
        scores = lax.dot_general(q, k_all, nt, preferred_element_type=jnp.float32) * scale
        scores = jnp.where(alive, scores, MASKED_SCORE)
        row_max = jnp.max(scores, axis=-1, keepdims=True)
        exp_scores = jnp.exp(scores - row_max)
        probs = exp_scores / jnp.sum(exp_scores, axis=-1, keepdims=True)
        weights = probs.astype(jnp.bfloat16)
        slot_out = jnp.dot(weights, v_all, preferred_element_type=jnp.float32).astype(jnp.bfloat16)
        out_ref[w] = slot_out
        delta = jnp.sum(g.astype(jnp.float32) * slot_out.astype(jnp.float32), axis=-1, keepdims=True)
        grad_probs = lax.dot_general(g, v_all, nt, preferred_element_type=jnp.float32)
        grad_scores = (probs * (grad_probs - delta) * scale).astype(jnp.bfloat16)
        dq_ref[w] = jnp.dot(grad_scores, k_all, preferred_element_type=jnp.float32).astype(jnp.bfloat16)
        grad_k = lax.dot_general(grad_scores, q, tn, preferred_element_type=jnp.float32)
        grad_v = lax.dot_general(weights, g, tn, preferred_element_type=jnp.float32)
        for j in range(nb):
            dk_ref[ids[j]] += grad_k[j * WIN : (j + 1) * WIN]
            dv_ref[ids[j]] += grad_v[j * WIN : (j + 1) * WIN]
        return carry

    lax.fori_loop(0, windows_n, body, 0)


def window_attention(key_index, length_ext, query_win, k_ext, v_ext, grad_win):
    windows_n, _, width = query_win.shape
    ext_n = k_ext.shape[0]
    keys = (key_index.shape[0] // windows_n) * WIN
    flops = 2 * windows_n * WIN * keys * width * 7
    vmem = pl.BlockSpec(memory_space=pltpu.VMEM)
    smem = pl.BlockSpec(memory_space=pltpu.SMEM)
    return pl.pallas_call(
        attention_kernel,
        out_shape=(
            jax.ShapeDtypeStruct(query_win.shape, jnp.bfloat16),
            jax.ShapeDtypeStruct(query_win.shape, jnp.bfloat16),
            jax.ShapeDtypeStruct((ext_n, WIN, width), jnp.float32),
            jax.ShapeDtypeStruct((ext_n, WIN, width), jnp.float32),
        ),
        in_specs=[smem, smem, vmem, vmem, vmem, vmem],
        out_specs=(vmem, vmem, vmem, vmem),
        compiler_params=pltpu.CompilerParams(vmem_limit_bytes=48 * 1024 * 1024),
        cost_estimate=pl.CostEstimate(
            flops=flops, transcendentals=windows_n * WIN * keys, bytes_accessed=8 * 1024 * 1024
        ),
    )(key_index, length_ext, query_win, k_ext, v_ext, grad_win)


def shards(query_feats, key_feats, value_feats, grad_output, lengths, members, neighbours):
    group_idx = lax.axis_index("space")
    groups = lax.axis_size("space")
    windows_n = members.shape[0]
    border = windows_n // 6
    per_block = 8
    block_count = windows_n // per_block
    col_width = query_feats.shape[1] // lax.axis_size("seq")
    head_count = col_width // HEAD
    own_length = lax.dynamic_index_in_dim(lengths, group_idx, 0, keepdims=False)
    before_length = lax.dynamic_index_in_dim(
        lengths, jnp.maximum(group_idx - 1, 0), 0, keepdims=False
    )
    after_length = lax.dynamic_index_in_dim(
        lengths, jnp.minimum(group_idx + 1, groups - 1), 0, keepdims=False
    )
    length_ext = jnp.concatenate(
        [
            jnp.where(group_idx > 0, before_length[windows_n - border :], 0),
            own_length,
            jnp.where(group_idx < groups - 1, after_length[:border], 0),
        ]
    )
    slot_alive = jnp.arange(WIN, dtype=jnp.int32)[None, :] < own_length[:, None]
    rows = query_feats.shape[0]
    seq_n = lax.axis_size("seq")
    stacked = jnp.stack(
        [
            jnp.transpose(part.reshape(rows, seq_n, col_width), (1, 0, 2))
            for part in (query_feats, key_feats, value_feats, grad_output)
        ],
        axis=2,
    ).reshape(seq_n, rows, 4 * col_width)
    heads_all = lax.all_to_all(stacked, "seq", split_axis=0, concat_axis=0, tiled=True)
    voxel_count = seq_n * rows
    table = heads_all.reshape(voxel_count, 4 * col_width)
    flat_slots = jnp.where(slot_alive, members, voxel_count).reshape(-1)
    slot_of = (
        jnp.zeros((voxel_count,), jnp.int32)
        .at[flat_slots]
        .set(jnp.arange(windows_n * WIN, dtype=jnp.int32), mode="drop")
    )

    def to_voxels(slot_vals):
        return gather_rows(slot_vals.reshape(windows_n * WIN, -1), slot_of)

    win_all = gather_rows(table, members)
    query_win = win_all[..., :col_width]
    kv_win = win_all[..., col_width : 3 * col_width]
    grad_win = win_all[..., 3 * col_width :] * slot_alive[:, :, None].astype(jnp.bfloat16)
    received = padded(border_rows(kv_win, border), (("space", 0),), border)
    kv_ext = extend_windows(kv_win, received, border)

    key_index = jnp.concatenate(
        [border + jnp.arange(windows_n, dtype=jnp.int32)[:, None], neighbours], axis=1
    ).reshape(-1)
    k_ext = kv_ext[..., :col_width]
    v_ext = kv_ext[..., col_width:]
    out_slots, grad_query_blocks, dk_ext, dv_ext = window_attention(
        key_index, length_ext, query_win, k_ext, v_ext, grad_win
    )
    grad_ext = jnp.concatenate([dk_ext, dv_ext], axis=-1)
    received_grads = padded(
        border_rows(grad_ext, border).astype(jnp.bfloat16), (("space", 0),), border
    ).astype(jnp.float32)
    own_grads = grad_ext[border : border + windows_n]
    own_grads = own_grads.at[:border].add(received_grads[:border])
    own_grads = own_grads.at[windows_n - border :].add(received_grads[3 * border :])
    slot_vals = jnp.concatenate(
        [out_slots, grad_query_blocks, own_grads.astype(jnp.bfloat16)], axis=-1
    )
    vox = to_voxels(slot_vals).reshape(seq_n, rows, 4 * col_width)
    back = lax.all_to_all(vox, "seq", split_axis=0, concat_axis=0, tiled=True)
    back = back.reshape(seq_n, rows, 4, col_width)
    return tuple(
        jnp.transpose(back[:, :, i], (1, 0, 2)).reshape(rows, seq_n * col_width) for i in range(4)
    )


def solution(mesh):
    in_specs = (
        P(("space", "seq"), None),
        P(("space", "seq"), None),
        P(("space", "seq"), None),
        P(("space", "seq"), None),
        P(),
        P("space", None),
        P("space", None),
    )
    out_specs = (
        P(("space", "seq"), None),
        P(("space", "seq"), None),
        P(("space", "seq"), None),
        P(("space", "seq"), None),
    )
    return jax.shard_map(shards, mesh=mesh, in_specs=in_specs, out_specs=out_specs, check_vma=False)
```

```python
import jax
import jax.numpy as jnp
from jax import lax
from jax.experimental import pallas as pl
from jax.experimental.pallas import tpu as pltpu
from jax.sharding import PartitionSpec as P

HEAD = 64
WIN = 64


MASKED_SCORE = -1e30


def padded(value, sides, width):
    for axis, dim in sides:
        count, length = (lax.axis_size(axis), value.shape[dim])
        up = [(i, (i + 1) % count) for i in range(count - 1)]
        down = [(j, i) for i, j in up]
        last = lax.slice_in_dim(value, length - width, length, axis=dim)
        first = lax.slice_in_dim(value, 0, width, axis=dim)
        before = lax.ppermute(last, axis, up)
        after = lax.ppermute(first, axis, down)
        value = jnp.concatenate([before, value, after], axis=dim)
    return value


def gather_rows(source, indices):
    return jnp.take(source, indices, axis=0)


def to_windows(query_part, key_part, value_part, members):
    query_win = gather_rows(query_part, members)
    kv_win = gather_rows(jnp.concatenate([key_part, value_part], axis=1), members)
    return (query_win, kv_win)


def border_rows(source, border):
    return jnp.concatenate([source[:border], source[source.shape[0] - border :]], axis=0)


def extend_windows(kv_win, received, border):
    return jnp.concatenate([received[:border], kv_win, received[3 * border :]], axis=0)


def window_keys(block_id, per_block, border, neighbours):
    start_row = block_id * per_block
    own_rows = border + start_row + jnp.arange(per_block, dtype=jnp.int32)
    near_rows = lax.dynamic_slice_in_dim(neighbours, start_row, per_block, 0)
    return jnp.concatenate([own_rows[:, None], near_rows], axis=1)


def block_attention(query_blk, key_index, kv_ext, length_ext, head_count):
    block_n = query_blk.shape[0]
    col_width = query_blk.shape[-1]
    head_size = col_width // head_count
    key_rows = gather_rows(kv_ext, key_index).reshape(block_n, -1, 2 * col_width)
    key_length = gather_rows(length_ext, key_index)
    key_alive = (jnp.arange(WIN, dtype=jnp.int32)[None, None, :] < key_length[:, :, None]).reshape(
        block_n, -1
    )
    query_heads = query_blk.reshape(block_n, WIN, head_count, head_size)
    key_heads = key_rows[:, :, :col_width].reshape(block_n, -1, head_count, head_size)
    value_heads = key_rows[:, :, col_width:].reshape(block_n, -1, head_count, head_size)
    score_scale = head_size ** (-0.5)
    scores = (
        jnp.einsum("wqhd,wkhd->whqk", query_heads, key_heads, preferred_element_type=jnp.float32)
        * score_scale
    )
    scores = jnp.where(key_alive[:, None, None, :], scores, MASKED_SCORE)
    row_max = jnp.max(scores, axis=-1, keepdims=True)
    exp_scores = jnp.exp(scores - row_max)
    attn_probs = exp_scores / jnp.sum(exp_scores, axis=-1, keepdims=True)
    return (attn_probs, query_heads, key_heads, value_heads, score_scale)


def attention_kernel(idx_ref, len_ref, qg_ref, kv_ref, out_ref, dkv_ref):
    windows_n, _, lanes = qg_ref.shape
    width = lanes // 2
    nb = idx_ref.shape[0] // windows_n
    keys = nb * WIN
    scale = HEAD ** (-0.5)
    dkv_ref[...] = jnp.zeros(dkv_ref.shape, dkv_ref.dtype)
    col = lax.broadcasted_iota(jnp.int32, (1, keys), 1)
    col_block = col // WIN
    col_slot = col % WIN
    lane = lax.broadcasted_iota(jnp.int32, (1, lanes), 1)
    first_half = lane < width
    nt = (((1,), (1,)), ((), ()))
    tn = (((0,), (0,)), ((), ()))

    def body(w, carry):
        ids = [idx_ref[w * nb + j] for j in range(nb)]
        qg = qg_ref[w]
        zero = jnp.zeros_like(qg)
        q_pad = jnp.where(first_half, qg, zero)
        g_pad = jnp.where(first_half, zero, qg)
        qg_blocks = jnp.concatenate([q_pad, g_pad], axis=0)
        kv_all = jnp.concatenate([kv_ref[i] for i in ids], axis=0)
        limit = jnp.zeros((1, keys), jnp.int32)
        for j in range(nb):
            limit = jnp.where(col_block == j, len_ref[ids[j]], limit)
        alive = col_slot < limit
        both = lax.dot_general(qg_blocks, kv_all, nt, preferred_element_type=jnp.float32)
        scores = both[:WIN] * scale
        grad_probs = both[WIN:]
        scores = jnp.where(alive, scores, MASKED_SCORE)
        row_max = jnp.max(scores, axis=-1, keepdims=True)
        exp_scores = jnp.exp(scores - row_max)
        probs = exp_scores / jnp.sum(exp_scores, axis=-1, keepdims=True)
        weights = probs.astype(jnp.bfloat16)
        out_full = jnp.dot(weights, kv_all, preferred_element_type=jnp.float32).astype(jnp.bfloat16)
        delta = jnp.sum(
            g_pad.astype(jnp.float32) * out_full.astype(jnp.float32), axis=-1, keepdims=True
        )
        grad_scores = (probs * (grad_probs - delta) * scale).astype(jnp.bfloat16)
        dq_full = jnp.dot(grad_scores, kv_all, preferred_element_type=jnp.float32).astype(jnp.bfloat16)
        out_ref[w] = jnp.where(first_half, dq_full, out_full)
        score_blocks = jnp.concatenate([grad_scores, weights], axis=0)
        grad_kv = lax.dot_general(score_blocks, qg_blocks, tn, preferred_element_type=jnp.float32)
        for j in range(nb):
            dkv_ref[ids[j]] += grad_kv[j * WIN : (j + 1) * WIN]
        return carry

    lax.fori_loop(0, windows_n, body, 0, unroll=2)


def window_attention(key_index, length_ext, qg_win, kv_ext):
    windows_n, _, lanes = qg_win.shape
    ext_n = kv_ext.shape[0]
    keys = (key_index.shape[0] // windows_n) * WIN
    flops = 2 * windows_n * WIN * keys * lanes * 6
    vmem = pl.BlockSpec(memory_space=pltpu.VMEM)
    smem = pl.BlockSpec(memory_space=pltpu.SMEM)
    return pl.pallas_call(
        attention_kernel,
        out_shape=(
            jax.ShapeDtypeStruct(qg_win.shape, jnp.bfloat16),
            jax.ShapeDtypeStruct((ext_n, WIN, lanes), jnp.float32),
        ),
        in_specs=[smem, smem, vmem, vmem],
        out_specs=(vmem, vmem),
        compiler_params=pltpu.CompilerParams(vmem_limit_bytes=48 * 1024 * 1024),
        cost_estimate=pl.CostEstimate(
            flops=flops, transcendentals=windows_n * WIN * keys, bytes_accessed=8 * 1024 * 1024
        ),
    )(key_index, length_ext, qg_win, kv_ext)


def shards(query_feats, key_feats, value_feats, grad_output, lengths, members, neighbours):
    group_idx = lax.axis_index("space")
    groups = lax.axis_size("space")
    windows_n = members.shape[0]
    border = windows_n // 6
    per_block = 8
    block_count = windows_n // per_block
    col_width = query_feats.shape[1] // lax.axis_size("seq")
    head_count = col_width // HEAD
    own_length = lax.dynamic_index_in_dim(lengths, group_idx, 0, keepdims=False)
    before_length = lax.dynamic_index_in_dim(
        lengths, jnp.maximum(group_idx - 1, 0), 0, keepdims=False
    )
    after_length = lax.dynamic_index_in_dim(
        lengths, jnp.minimum(group_idx + 1, groups - 1), 0, keepdims=False
    )
    length_ext = jnp.concatenate(
        [
            jnp.where(group_idx > 0, before_length[windows_n - border :], 0),
            own_length,
            jnp.where(group_idx < groups - 1, after_length[:border], 0),
        ]
    )
    slot_alive = jnp.arange(WIN, dtype=jnp.int32)[None, :] < own_length[:, None]
    rows = query_feats.shape[0]
    seq_n = lax.axis_size("seq")
    stacked = jnp.stack(
        [
            jnp.transpose(part.reshape(rows, seq_n, col_width), (1, 0, 2))
            for part in (query_feats, grad_output, key_feats, value_feats)
        ],
        axis=2,
    ).reshape(seq_n, rows, 4 * col_width)
    heads_all = lax.all_to_all(stacked, "seq", split_axis=0, concat_axis=0, tiled=True)
    voxel_count = seq_n * rows
    table = heads_all.reshape(voxel_count, 4 * col_width)
    flat_slots = jnp.where(slot_alive, members, voxel_count).reshape(-1)
    slot_of = (
        jnp.zeros((voxel_count,), jnp.int32)
        .at[flat_slots]
        .set(jnp.arange(windows_n * WIN, dtype=jnp.int32), mode="drop")
    )

    def to_voxels(slot_vals):
        return gather_rows(slot_vals.reshape(windows_n * WIN, -1), slot_of)

    win_all = gather_rows(table, members)
    lane_live = jnp.logical_or(
        jnp.arange(2 * col_width, dtype=jnp.int32)[None, None, :] < col_width,
        slot_alive[:, :, None],
    )
    qg_win = win_all[..., : 2 * col_width] * lane_live.astype(jnp.bfloat16)
    kv_win = win_all[..., 2 * col_width :]
    received = padded(border_rows(kv_win, border), (("space", 0),), border)
    kv_ext = extend_windows(kv_win, received, border)

    key_index = jnp.concatenate(
        [border + jnp.arange(windows_n, dtype=jnp.int32)[:, None], neighbours], axis=1
    ).reshape(-1)
    dq_out, grad_ext = window_attention(key_index, length_ext, qg_win, kv_ext)
    received_grads = padded(
        border_rows(grad_ext, border).astype(jnp.bfloat16), (("space", 0),), border
    ).astype(jnp.float32)
    own_grads = grad_ext[border : border + windows_n]
    own_grads = own_grads.at[:border].add(received_grads[:border])
    own_grads = own_grads.at[windows_n - border :].add(received_grads[3 * border :])
    slot_vals = jnp.concatenate(
        [dq_out, own_grads.astype(jnp.bfloat16)], axis=-1
    )
    vox = to_voxels(slot_vals).reshape(seq_n, rows, 4 * col_width)
    back = lax.all_to_all(vox, "seq", split_axis=0, concat_axis=0, tiled=True)
    back = back.reshape(seq_n, rows, 4, col_width)
    results = [
        jnp.transpose(back[:, :, i], (1, 0, 2)).reshape(rows, seq_n * col_width) for i in range(4)
    ]
    return (results[1], results[0], results[2], results[3])


def solution(mesh):
    in_specs = (
        P(("space", "seq"), None),
        P(("space", "seq"), None),
        P(("space", "seq"), None),
        P(("space", "seq"), None),
        P(),
        P("space", None),
        P("space", None),
    )
    out_specs = (
        P(("space", "seq"), None),
        P(("space", "seq"), None),
        P(("space", "seq"), None),
        P(("space", "seq"), None),
    )
    return jax.shard_map(shards, mesh=mesh, in_specs=in_specs, out_specs=out_specs, check_vma=False)
```

```python
import jax
import jax.numpy as jnp
from jax import lax
from jax.experimental import pallas as pl
from jax.experimental.pallas import tpu as pltpu
from jax.sharding import PartitionSpec as P

HEAD = 64
WIN = 64


MASKED_SCORE = -1e30


def padded(value, sides, width):
    for axis, dim in sides:
        count, length = (lax.axis_size(axis), value.shape[dim])
        up = [(i, (i + 1) % count) for i in range(count - 1)]
        down = [(j, i) for i, j in up]
        last = lax.slice_in_dim(value, length - width, length, axis=dim)
        first = lax.slice_in_dim(value, 0, width, axis=dim)
        before = lax.ppermute(last, axis, up)
        after = lax.ppermute(first, axis, down)
        value = jnp.concatenate([before, value, after], axis=dim)
    return value


def gather_rows(source, indices):
    return jnp.take(source, indices, axis=0)


def to_windows(query_part, key_part, value_part, members):
    query_win = gather_rows(query_part, members)
    kv_win = gather_rows(jnp.concatenate([key_part, value_part], axis=1), members)
    return (query_win, kv_win)


def border_rows(source, border):
    return jnp.concatenate([source[:border], source[source.shape[0] - border :]], axis=0)


def extend_windows(kv_win, received, border):
    return jnp.concatenate([received[:border], kv_win, received[3 * border :]], axis=0)


def window_keys(block_id, per_block, border, neighbours):
    start_row = block_id * per_block
    own_rows = border + start_row + jnp.arange(per_block, dtype=jnp.int32)
    near_rows = lax.dynamic_slice_in_dim(neighbours, start_row, per_block, 0)
    return jnp.concatenate([own_rows[:, None], near_rows], axis=1)


def block_attention(query_blk, key_index, kv_ext, length_ext, head_count):
    block_n = query_blk.shape[0]
    col_width = query_blk.shape[-1]
    head_size = col_width // head_count
    key_rows = gather_rows(kv_ext, key_index).reshape(block_n, -1, 2 * col_width)
    key_length = gather_rows(length_ext, key_index)
    key_alive = (jnp.arange(WIN, dtype=jnp.int32)[None, None, :] < key_length[:, :, None]).reshape(
        block_n, -1
    )
    query_heads = query_blk.reshape(block_n, WIN, head_count, head_size)
    key_heads = key_rows[:, :, :col_width].reshape(block_n, -1, head_count, head_size)
    value_heads = key_rows[:, :, col_width:].reshape(block_n, -1, head_count, head_size)
    score_scale = head_size ** (-0.5)
    scores = (
        jnp.einsum("wqhd,wkhd->whqk", query_heads, key_heads, preferred_element_type=jnp.float32)
        * score_scale
    )
    scores = jnp.where(key_alive[:, None, None, :], scores, MASKED_SCORE)
    row_max = jnp.max(scores, axis=-1, keepdims=True)
    exp_scores = jnp.exp(scores - row_max)
    attn_probs = exp_scores / jnp.sum(exp_scores, axis=-1, keepdims=True)
    return (attn_probs, query_heads, key_heads, value_heads, score_scale)


def attention_kernel(idx_ref, len_ref, win_ref, kv_ref, out_ref, dkv_ref):
    windows_n = win_ref.shape[0]
    lanes = kv_ref.shape[-1]
    width = lanes // 2
    nb = idx_ref.shape[0] // windows_n
    keys = nb * WIN
    scale = HEAD ** (-0.5)
    dkv_ref[...] = jnp.zeros(dkv_ref.shape, dkv_ref.dtype)
    col = lax.broadcasted_iota(jnp.int32, (1, keys), 1)
    col_block = col // WIN
    col_slot = col % WIN
    lane = lax.broadcasted_iota(jnp.int32, (1, lanes), 1)
    first_half = lane < width
    slot_row = lax.broadcasted_iota(jnp.int32, (WIN, 1), 0)
    nt = (((1,), (1,)), ((), ()))
    tn = (((0,), (0,)), ((), ()))

    def body(w, carry):
        ids = [idx_ref[w * nb + j] for j in range(nb)]
        qg = win_ref[w, :, :lanes]
        zero = jnp.zeros_like(qg)
        q_pad = jnp.where(first_half, qg, zero)
        g_live = jnp.logical_and(jnp.logical_not(first_half), slot_row < len_ref[ids[0]])
        g_pad = jnp.where(g_live, qg, zero)
        qg_blocks = jnp.concatenate([q_pad, g_pad], axis=0)
        kv_all = jnp.concatenate([kv_ref[i] for i in ids], axis=0)
        limit = jnp.zeros((1, keys), jnp.int32)
        for j in range(nb):
            limit = jnp.where(col_block == j, len_ref[ids[j]], limit)
        alive = col_slot < limit
        both = lax.dot_general(qg_blocks, kv_all, nt, preferred_element_type=jnp.float32)
        scores = both[:WIN] * scale
        grad_probs = both[WIN:]
        scores = jnp.where(alive, scores, MASKED_SCORE)
        row_max = jnp.max(scores, axis=-1, keepdims=True)
        exp_scores = jnp.exp(scores - row_max)
        probs = exp_scores / jnp.sum(exp_scores, axis=-1, keepdims=True)
        weights = probs.astype(jnp.bfloat16)
        out_full = jnp.dot(weights, kv_all, preferred_element_type=jnp.float32).astype(jnp.bfloat16)
        delta = jnp.sum(
            g_pad.astype(jnp.float32) * out_full.astype(jnp.float32), axis=-1, keepdims=True
        )
        grad_scores = (probs * (grad_probs - delta) * scale).astype(jnp.bfloat16)
        dq_full = jnp.dot(grad_scores, kv_all, preferred_element_type=jnp.float32).astype(jnp.bfloat16)
        out_ref[w] = jnp.where(first_half, dq_full, out_full)
        score_blocks = jnp.concatenate([grad_scores, weights], axis=0)
        grad_kv = lax.dot_general(score_blocks, qg_blocks, tn, preferred_element_type=jnp.float32)
        for j in range(nb):
            dkv_ref[ids[j]] += grad_kv[j * WIN : (j + 1) * WIN]
        return carry

    lax.fori_loop(0, windows_n, body, 0, unroll=8)


def window_attention(key_index, length_ext, win_all, kv_ext):
    windows_n = win_all.shape[0]
    lanes = kv_ext.shape[-1]
    ext_n = kv_ext.shape[0]
    keys = (key_index.shape[0] // windows_n) * WIN
    flops = 2 * windows_n * WIN * keys * lanes * 6
    vmem = pl.BlockSpec(memory_space=pltpu.VMEM)
    smem = pl.BlockSpec(memory_space=pltpu.SMEM)
    return pl.pallas_call(
        attention_kernel,
        out_shape=(
            jax.ShapeDtypeStruct((windows_n, WIN, lanes), jnp.bfloat16),
            jax.ShapeDtypeStruct((ext_n, WIN, lanes), jnp.float32),
        ),
        in_specs=[smem, smem, vmem, vmem],
        out_specs=(vmem, vmem),
        compiler_params=pltpu.CompilerParams(vmem_limit_bytes=48 * 1024 * 1024),
        cost_estimate=pl.CostEstimate(
            flops=flops, transcendentals=windows_n * WIN * keys, bytes_accessed=8 * 1024 * 1024
        ),
    )(key_index, length_ext, win_all, kv_ext)


def shards(query_feats, key_feats, value_feats, grad_output, lengths, members, neighbours):
    group_idx = lax.axis_index("space")
    groups = lax.axis_size("space")
    windows_n = members.shape[0]
    border = windows_n // 6
    per_block = 8
    block_count = windows_n // per_block
    col_width = query_feats.shape[1] // lax.axis_size("seq")
    head_count = col_width // HEAD
    own_length = lax.dynamic_index_in_dim(lengths, group_idx, 0, keepdims=False)
    before_length = lax.dynamic_index_in_dim(
        lengths, jnp.maximum(group_idx - 1, 0), 0, keepdims=False
    )
    after_length = lax.dynamic_index_in_dim(
        lengths, jnp.minimum(group_idx + 1, groups - 1), 0, keepdims=False
    )
    length_ext = jnp.concatenate(
        [
            jnp.where(group_idx > 0, before_length[windows_n - border :], 0),
            own_length,
            jnp.where(group_idx < groups - 1, after_length[:border], 0),
        ]
    )
    slot_alive = jnp.arange(WIN, dtype=jnp.int32)[None, :] < own_length[:, None]
    rows = query_feats.shape[0]
    seq_n = lax.axis_size("seq")
    stacked = jnp.stack(
        [
            jnp.transpose(part.reshape(rows, seq_n, col_width), (1, 0, 2))
            for part in (query_feats, grad_output, key_feats, value_feats)
        ],
        axis=2,
    ).reshape(seq_n, rows, 4 * col_width)
    heads_all = lax.all_to_all(stacked, "seq", split_axis=0, concat_axis=0, tiled=True)
    voxel_count = seq_n * rows
    table = heads_all.reshape(voxel_count, 4 * col_width)
    flat_slots = jnp.where(slot_alive, members, voxel_count).reshape(-1)
    slot_of = (
        jnp.zeros((voxel_count,), jnp.int32)
        .at[flat_slots]
        .set(jnp.arange(windows_n * WIN, dtype=jnp.int32), mode="drop")
    )

    def to_voxels(slot_vals):
        return gather_rows(slot_vals.reshape(windows_n * WIN, -1), slot_of)

    win_all = gather_rows(table, members)
    kv_win = win_all[..., 2 * col_width :]
    received = padded(border_rows(kv_win, border), (("space", 0),), border)
    kv_ext = extend_windows(kv_win, received, border)

    key_index = jnp.concatenate(
        [border + jnp.arange(windows_n, dtype=jnp.int32)[:, None], neighbours], axis=1
    ).reshape(-1)
    dq_out, grad_ext = window_attention(key_index, length_ext, win_all, kv_ext)
    received_grads = padded(
        border_rows(grad_ext, border).astype(jnp.bfloat16), (("space", 0),), border
    ).astype(jnp.float32)
    own_grads = grad_ext[border : border + windows_n]
    own_grads = own_grads.at[:border].add(received_grads[:border])
    own_grads = own_grads.at[windows_n - border :].add(received_grads[3 * border :])
    slot_vals = jnp.concatenate(
        [dq_out, own_grads.astype(jnp.bfloat16)], axis=-1
    )
    vox = to_voxels(slot_vals).reshape(seq_n, rows, 4 * col_width)
    back = lax.all_to_all(vox, "seq", split_axis=0, concat_axis=0, tiled=True)
    back = back.reshape(seq_n, rows, 4, col_width)
    results = [
        jnp.transpose(back[:, :, i], (1, 0, 2)).reshape(rows, seq_n * col_width) for i in range(4)
    ]
    return (results[1], results[0], results[2], results[3])


def solution(mesh):
    in_specs = (
        P(("space", "seq"), None),
        P(("space", "seq"), None),
        P(("space", "seq"), None),
        P(("space", "seq"), None),
        P(),
        P("space", None),
        P("space", None),
    )
    out_specs = (
        P(("space", "seq"), None),
        P(("space", "seq"), None),
        P(("space", "seq"), None),
        P(("space", "seq"), None),
    )
    return jax.shard_map(shards, mesh=mesh, in_specs=in_specs, out_specs=out_specs, check_vma=False)
```

```python
import functools

import jax
import jax.numpy as jnp
from jax import lax
from jax.experimental import pallas as pl
from jax.experimental.pallas import tpu as pltpu
from jax.sharding import PartitionSpec as P

HEAD = 64
WIN = 64


MASKED_SCORE = -1e30


def padded(value, sides, width):
    for axis, dim in sides:
        count, length = (lax.axis_size(axis), value.shape[dim])
        up = [(i, (i + 1) % count) for i in range(count - 1)]
        down = [(j, i) for i, j in up]
        last = lax.slice_in_dim(value, length - width, length, axis=dim)
        first = lax.slice_in_dim(value, 0, width, axis=dim)
        before = lax.ppermute(last, axis, up)
        after = lax.ppermute(first, axis, down)
        value = jnp.concatenate([before, value, after], axis=dim)
    return value


def gather_rows(source, indices):
    return jnp.take(source, indices, axis=0)


def to_windows(query_part, key_part, value_part, members):
    query_win = gather_rows(query_part, members)
    kv_win = gather_rows(jnp.concatenate([key_part, value_part], axis=1), members)
    return (query_win, kv_win)


def border_rows(source, border):
    return jnp.concatenate([source[:border], source[source.shape[0] - border :]], axis=0)


def extend_windows(kv_win, received, border):
    return jnp.concatenate([received[:border], kv_win, received[3 * border :]], axis=0)


def window_keys(block_id, per_block, border, neighbours):
    start_row = block_id * per_block
    own_rows = border + start_row + jnp.arange(per_block, dtype=jnp.int32)
    near_rows = lax.dynamic_slice_in_dim(neighbours, start_row, per_block, 0)
    return jnp.concatenate([own_rows[:, None], near_rows], axis=1)


def block_attention(query_blk, key_index, kv_ext, length_ext, head_count):
    block_n = query_blk.shape[0]
    col_width = query_blk.shape[-1]
    head_size = col_width // head_count
    key_rows = gather_rows(kv_ext, key_index).reshape(block_n, -1, 2 * col_width)
    key_length = gather_rows(length_ext, key_index)
    key_alive = (jnp.arange(WIN, dtype=jnp.int32)[None, None, :] < key_length[:, :, None]).reshape(
        block_n, -1
    )
    query_heads = query_blk.reshape(block_n, WIN, head_count, head_size)
    key_heads = key_rows[:, :, :col_width].reshape(block_n, -1, head_count, head_size)
    value_heads = key_rows[:, :, col_width:].reshape(block_n, -1, head_count, head_size)
    score_scale = head_size ** (-0.5)
    scores = (
        jnp.einsum("wqhd,wkhd->whqk", query_heads, key_heads, preferred_element_type=jnp.float32)
        * score_scale
    )
    scores = jnp.where(key_alive[:, None, None, :], scores, MASKED_SCORE)
    row_max = jnp.max(scores, axis=-1, keepdims=True)
    exp_scores = jnp.exp(scores - row_max)
    attn_probs = exp_scores / jnp.sum(exp_scores, axis=-1, keepdims=True)
    return (attn_probs, query_heads, key_heads, value_heads, score_scale)


def attention_kernel(ranges, kv_offset, fresh, idx_ref, len_ref, win_ref, kv_ref, *refs):
    out_ref, dkv_ref = refs[-2:]
    windows_n = win_ref.shape[0]
    lanes = kv_ref.shape[-1]
    width = lanes // 2
    nb = idx_ref.shape[0] // windows_n
    keys = nb * WIN
    scale = HEAD ** (-0.5)
    if fresh:
        dkv_ref[...] = jnp.zeros(dkv_ref.shape, dkv_ref.dtype)
    else:
        out_ref[...] = refs[0][...]
        dkv_ref[...] = refs[1][...]
    col = lax.broadcasted_iota(jnp.int32, (1, keys), 1)
    col_block = col // WIN
    col_slot = col % WIN
    lane = lax.broadcasted_iota(jnp.int32, (1, lanes), 1)
    first_half = lane < width
    slot_row = lax.broadcasted_iota(jnp.int32, (WIN, 1), 0)
    nt = (((1,), (1,)), ((), ()))
    tn = (((0,), (0,)), ((), ()))

    def body(w, carry):
        ids = [idx_ref[w * nb + j] for j in range(nb)]
        qg = win_ref[w, :, :lanes]
        zero = jnp.zeros_like(qg)
        q_pad = jnp.where(first_half, qg, zero)
        g_live = jnp.logical_and(jnp.logical_not(first_half), slot_row < len_ref[ids[0]])
        g_pad = jnp.where(g_live, qg, zero)
        qg_blocks = jnp.concatenate([q_pad, g_pad], axis=0)
        kv_all = jnp.concatenate([kv_ref[i - kv_offset] for i in ids], axis=0)
        limit = jnp.zeros((1, keys), jnp.int32)
        for j in range(nb):
            limit = jnp.where(col_block == j, len_ref[ids[j]], limit)
        alive = col_slot < limit
        both = lax.dot_general(qg_blocks, kv_all, nt, preferred_element_type=jnp.float32)
        scores = both[:WIN] * scale
        grad_probs = both[WIN:]
        scores = jnp.where(alive, scores, MASKED_SCORE)
        row_max = jnp.max(scores, axis=-1, keepdims=True)
        exp_scores = jnp.exp(scores - row_max)
        probs = exp_scores / jnp.sum(exp_scores, axis=-1, keepdims=True)
        weights = probs.astype(jnp.bfloat16)
        out_full = jnp.dot(weights, kv_all, preferred_element_type=jnp.float32).astype(jnp.bfloat16)
        delta = jnp.sum(
            g_pad.astype(jnp.float32) * out_full.astype(jnp.float32), axis=-1, keepdims=True
        )
        grad_scores = (probs * (grad_probs - delta) * scale).astype(jnp.bfloat16)
        dq_full = jnp.dot(grad_scores, kv_all, preferred_element_type=jnp.float32).astype(jnp.bfloat16)
        out_ref[w] = jnp.where(first_half, dq_full, out_full)
        score_blocks = jnp.concatenate([grad_scores, weights], axis=0)
        grad_kv = lax.dot_general(score_blocks, qg_blocks, tn, preferred_element_type=jnp.float32)
        for j in range(nb):
            dkv_ref[ids[j]] += grad_kv[j * WIN : (j + 1) * WIN]
        return carry

    for start, stop in ranges:
        lax.fori_loop(start, stop, body, 0, unroll=8)


def window_attention(ranges, kv_offset, key_index, length_ext, win_all, kv_part, carried=None):
    windows_n = win_all.shape[0]
    lanes = kv_part.shape[-1]
    ext_n = length_ext.shape[0]
    keys = (key_index.shape[0] // windows_n) * WIN
    count = sum(stop - start for start, stop in ranges)
    flops = 2 * count * WIN * keys * lanes * 6
    vmem = pl.BlockSpec(memory_space=pltpu.VMEM)
    smem = pl.BlockSpec(memory_space=pltpu.SMEM)
    operands = [key_index, length_ext, win_all, kv_part]
    aliases = {}
    if carried is not None:
        operands += list(carried)
        aliases = {4: 0, 5: 1}
    kernel = functools.partial(attention_kernel, tuple(ranges), kv_offset, carried is None)
    return pl.pallas_call(
        kernel,
        out_shape=(
            jax.ShapeDtypeStruct((windows_n, WIN, lanes), jnp.bfloat16),
            jax.ShapeDtypeStruct((ext_n, WIN, lanes), jnp.float32),
        ),
        in_specs=[smem, smem] + [vmem] * (len(operands) - 2),
        out_specs=(vmem, vmem),
        input_output_aliases=aliases,
        compiler_params=pltpu.CompilerParams(vmem_limit_bytes=48 * 1024 * 1024),
        cost_estimate=pl.CostEstimate(
            flops=flops, transcendentals=count * WIN * keys, bytes_accessed=count * 96 * 1024
        ),
    )(*operands)


def shards(query_feats, key_feats, value_feats, grad_output, lengths, members, neighbours):
    group_idx = lax.axis_index("space")
    groups = lax.axis_size("space")
    windows_n = members.shape[0]
    border = windows_n // 6
    per_block = 8
    block_count = windows_n // per_block
    col_width = query_feats.shape[1] // lax.axis_size("seq")
    head_count = col_width // HEAD
    own_length = lax.dynamic_index_in_dim(lengths, group_idx, 0, keepdims=False)
    before_length = lax.dynamic_index_in_dim(
        lengths, jnp.maximum(group_idx - 1, 0), 0, keepdims=False
    )
    after_length = lax.dynamic_index_in_dim(
        lengths, jnp.minimum(group_idx + 1, groups - 1), 0, keepdims=False
    )
    length_ext = jnp.concatenate(
        [
            jnp.where(group_idx > 0, before_length[windows_n - border :], 0),
            own_length,
            jnp.where(group_idx < groups - 1, after_length[:border], 0),
        ]
    )
    slot_alive = jnp.arange(WIN, dtype=jnp.int32)[None, :] < own_length[:, None]
    rows = query_feats.shape[0]
    seq_n = lax.axis_size("seq")
    stacked = jnp.stack(
        [
            jnp.transpose(part.reshape(rows, seq_n, col_width), (1, 0, 2))
            for part in (query_feats, grad_output, key_feats, value_feats)
        ],
        axis=2,
    ).reshape(seq_n, rows, 4 * col_width)
    heads_all = lax.all_to_all(stacked, "seq", split_axis=0, concat_axis=0, tiled=True)
    voxel_count = seq_n * rows
    table = heads_all.reshape(voxel_count, 4 * col_width)
    flat_slots = jnp.where(slot_alive, members, voxel_count).reshape(-1)
    slot_of = (
        jnp.zeros((voxel_count,), jnp.int32)
        .at[flat_slots]
        .set(jnp.arange(windows_n * WIN, dtype=jnp.int32), mode="drop")
    )

    def to_voxels(slot_vals):
        return gather_rows(slot_vals.reshape(windows_n * WIN, -1), slot_of)

    win_all = gather_rows(table, members)
    kv_win = win_all[..., 2 * col_width :]
    received = padded(border_rows(kv_win, border), (("space", 0),), border)
    kv_ext = extend_windows(kv_win, received, border)

    key_index = jnp.concatenate(
        [border + jnp.arange(windows_n, dtype=jnp.int32)[:, None], neighbours], axis=1
    ).reshape(-1)
    kv_own = win_all[..., 2 * col_width :]
    middle = windows_n - 2 * border
    first_part = [(border, border + middle // 2)]
    rim_part = [(0, border), (windows_n - border, windows_n)]
    last_part = [(border + middle // 2, windows_n - border)]
    carried = window_attention(first_part, border, key_index, length_ext, win_all, kv_own)
    carried = window_attention(rim_part, 0, key_index, length_ext, win_all, kv_ext, carried)
    rim_grads = border_rows(carried[1], border).astype(jnp.bfloat16)
    dq_out, grad_ext = window_attention(
        last_part, border, key_index, length_ext, win_all, kv_own, carried
    )
    received_grads = padded(rim_grads, (("space", 0),), border).astype(jnp.float32)
    own_grads = grad_ext[border : border + windows_n]
    own_grads = own_grads.at[:border].add(received_grads[:border])
    own_grads = own_grads.at[windows_n - border :].add(received_grads[3 * border :])
    slot_vals = jnp.concatenate(
        [dq_out, own_grads.astype(jnp.bfloat16)], axis=-1
    )
    vox = to_voxels(slot_vals).reshape(seq_n, rows, 4 * col_width)
    back = lax.all_to_all(vox, "seq", split_axis=0, concat_axis=0, tiled=True)
    back = back.reshape(seq_n, rows, 4, col_width)
    results = [
        jnp.transpose(back[:, :, i], (1, 0, 2)).reshape(rows, seq_n * col_width) for i in range(4)
    ]
    return (results[1], results[0], results[2], results[3])


def solution(mesh):
    in_specs = (
        P(("space", "seq"), None),
        P(("space", "seq"), None),
        P(("space", "seq"), None),
        P(("space", "seq"), None),
        P(),
        P("space", None),
        P("space", None),
    )
    out_specs = (
        P(("space", "seq"), None),
        P(("space", "seq"), None),
        P(("space", "seq"), None),
        P(("space", "seq"), None),
    )
    return jax.shard_map(shards, mesh=mesh, in_specs=in_specs, out_specs=out_specs, check_vma=False)
```

```python
import jax
import jax.numpy as jnp
from jax import lax
from jax.experimental import pallas as pl
from jax.experimental.pallas import tpu as pltpu
from jax.sharding import PartitionSpec as P

HEAD = 64
WIN = 64


MASKED_SCORE = -1e30


def padded(value, sides, width):
    for axis, dim in sides:
        count, length = (lax.axis_size(axis), value.shape[dim])
        up = [(i, (i + 1) % count) for i in range(count - 1)]
        down = [(j, i) for i, j in up]
        last = lax.slice_in_dim(value, length - width, length, axis=dim)
        first = lax.slice_in_dim(value, 0, width, axis=dim)
        before = lax.ppermute(last, axis, up)
        after = lax.ppermute(first, axis, down)
        value = jnp.concatenate([before, value, after], axis=dim)
    return value


def gather_rows(source, indices):
    return source.at[indices].get(mode="promise_in_bounds")


def to_windows(query_part, key_part, value_part, members):
    query_win = gather_rows(query_part, members)
    kv_win = gather_rows(jnp.concatenate([key_part, value_part], axis=1), members)
    return (query_win, kv_win)


def border_rows(source, border):
    return jnp.concatenate([source[:border], source[source.shape[0] - border :]], axis=0)


def extend_windows(kv_win, received, border):
    return jnp.concatenate([received[:border], kv_win, received[3 * border :]], axis=0)


def window_keys(block_id, per_block, border, neighbours):
    start_row = block_id * per_block
    own_rows = border + start_row + jnp.arange(per_block, dtype=jnp.int32)
    near_rows = lax.dynamic_slice_in_dim(neighbours, start_row, per_block, 0)
    return jnp.concatenate([own_rows[:, None], near_rows], axis=1)


def block_attention(query_blk, key_index, kv_ext, length_ext, head_count):
    block_n = query_blk.shape[0]
    col_width = query_blk.shape[-1]
    head_size = col_width // head_count
    key_rows = gather_rows(kv_ext, key_index).reshape(block_n, -1, 2 * col_width)
    key_length = gather_rows(length_ext, key_index)
    key_alive = (jnp.arange(WIN, dtype=jnp.int32)[None, None, :] < key_length[:, :, None]).reshape(
        block_n, -1
    )
    query_heads = query_blk.reshape(block_n, WIN, head_count, head_size)
    key_heads = key_rows[:, :, :col_width].reshape(block_n, -1, head_count, head_size)
    value_heads = key_rows[:, :, col_width:].reshape(block_n, -1, head_count, head_size)
    score_scale = head_size ** (-0.5)
    scores = (
        jnp.einsum("wqhd,wkhd->whqk", query_heads, key_heads, preferred_element_type=jnp.float32)
        * score_scale
    )
    scores = jnp.where(key_alive[:, None, None, :], scores, MASKED_SCORE)
    row_max = jnp.max(scores, axis=-1, keepdims=True)
    exp_scores = jnp.exp(scores - row_max)
    attn_probs = exp_scores / jnp.sum(exp_scores, axis=-1, keepdims=True)
    return (attn_probs, query_heads, key_heads, value_heads, score_scale)


def attention_kernel(idx_ref, len_ref, win_ref, kv_ref, out_ref, dkv_ref):
    windows_n = win_ref.shape[0]
    lanes = kv_ref.shape[-1]
    width = lanes // 2
    nb = idx_ref.shape[0] // windows_n
    keys = nb * WIN
    scale = HEAD ** (-0.5)
    dkv_ref[...] = jnp.zeros(dkv_ref.shape, dkv_ref.dtype)
    col = lax.broadcasted_iota(jnp.int32, (1, keys), 1)
    col_block = col // WIN
    col_slot = col % WIN
    lane = lax.broadcasted_iota(jnp.int32, (1, lanes), 1)
    first_half = lane < width
    slot_row = lax.broadcasted_iota(jnp.int32, (WIN, 1), 0)
    nt = (((1,), (1,)), ((), ()))
    tn = (((0,), (0,)), ((), ()))

    def body(w, carry):
        ids = [idx_ref[w * nb + j] for j in range(nb)]
        qg = win_ref[w, :, :lanes]
        zero = jnp.zeros_like(qg)
        q_pad = jnp.where(first_half, qg, zero)
        g_live = jnp.logical_and(jnp.logical_not(first_half), slot_row < len_ref[ids[0]])
        g_pad = jnp.where(g_live, qg, zero)
        qg_blocks = jnp.concatenate([q_pad, g_pad], axis=0)
        kv_all = jnp.concatenate([kv_ref[i] for i in ids], axis=0)
        limit = jnp.zeros((1, keys), jnp.int32)
        for j in range(nb):
            limit = jnp.where(col_block == j, len_ref[ids[j]], limit)
        alive = col_slot < limit
        both = lax.dot_general(qg_blocks, kv_all, nt, preferred_element_type=jnp.float32)
        scores = both[:WIN] * scale
        grad_probs = both[WIN:]
        scores = jnp.where(alive, scores, MASKED_SCORE)
        row_max = jnp.max(scores, axis=-1, keepdims=True)
        exp_scores = jnp.exp(scores - row_max)
        probs = exp_scores / jnp.sum(exp_scores, axis=-1, keepdims=True)
        weights = probs.astype(jnp.bfloat16)
        out_full = jnp.dot(weights, kv_all, preferred_element_type=jnp.float32).astype(jnp.bfloat16)
        delta = jnp.sum(
            g_pad.astype(jnp.float32) * out_full.astype(jnp.float32), axis=-1, keepdims=True
        )
        grad_scores = (probs * (grad_probs - delta) * scale).astype(jnp.bfloat16)
        dq_full = jnp.dot(grad_scores, kv_all, preferred_element_type=jnp.float32).astype(jnp.bfloat16)
        out_ref[w] = jnp.where(first_half, dq_full, out_full)
        score_blocks = jnp.concatenate([grad_scores, weights], axis=0)
        grad_kv = lax.dot_general(score_blocks, qg_blocks, tn, preferred_element_type=jnp.float32)
        for j in range(nb):
            dkv_ref[ids[j]] += grad_kv[j * WIN : (j + 1) * WIN]
        return carry

    lax.fori_loop(0, windows_n, body, 0, unroll=8)


def window_attention(key_index, length_ext, win_all, kv_ext):
    windows_n = win_all.shape[0]
    lanes = kv_ext.shape[-1]
    ext_n = kv_ext.shape[0]
    keys = (key_index.shape[0] // windows_n) * WIN
    flops = 2 * windows_n * WIN * keys * lanes * 6
    vmem = pl.BlockSpec(memory_space=pltpu.VMEM)
    smem = pl.BlockSpec(memory_space=pltpu.SMEM)
    return pl.pallas_call(
        attention_kernel,
        out_shape=(
            jax.ShapeDtypeStruct((windows_n, WIN, lanes), jnp.bfloat16),
            jax.ShapeDtypeStruct((ext_n, WIN, lanes), jnp.float32),
        ),
        in_specs=[smem, smem, vmem, vmem],
        out_specs=(vmem, vmem),
        compiler_params=pltpu.CompilerParams(vmem_limit_bytes=48 * 1024 * 1024),
        cost_estimate=pl.CostEstimate(
            flops=flops, transcendentals=windows_n * WIN * keys, bytes_accessed=8 * 1024 * 1024
        ),
    )(key_index, length_ext, win_all, kv_ext)


def shards(query_feats, key_feats, value_feats, grad_output, lengths, members, neighbours):
    group_idx = lax.axis_index("space")
    groups = lax.axis_size("space")
    windows_n = members.shape[0]
    border = windows_n // 6
    per_block = 8
    block_count = windows_n // per_block
    col_width = query_feats.shape[1] // lax.axis_size("seq")
    head_count = col_width // HEAD
    own_length = lax.dynamic_index_in_dim(lengths, group_idx, 0, keepdims=False)
    before_length = lax.dynamic_index_in_dim(
        lengths, jnp.maximum(group_idx - 1, 0), 0, keepdims=False
    )
    after_length = lax.dynamic_index_in_dim(
        lengths, jnp.minimum(group_idx + 1, groups - 1), 0, keepdims=False
    )
    length_ext = jnp.concatenate(
        [
            jnp.where(group_idx > 0, before_length[windows_n - border :], 0),
            own_length,
            jnp.where(group_idx < groups - 1, after_length[:border], 0),
        ]
    )
    slot_alive = jnp.arange(WIN, dtype=jnp.int32)[None, :] < own_length[:, None]
    rows = query_feats.shape[0]
    seq_n = lax.axis_size("seq")
    stacked = jnp.stack(
        [
            jnp.transpose(part.reshape(rows, seq_n, col_width), (1, 0, 2))
            for part in (query_feats, grad_output, key_feats, value_feats)
        ],
        axis=2,
    ).reshape(seq_n, rows, 4 * col_width)
    heads_all = lax.all_to_all(stacked, "seq", split_axis=0, concat_axis=0, tiled=True)
    voxel_count = seq_n * rows
    table = heads_all.reshape(voxel_count, 4 * col_width)
    flat_slots = jnp.where(slot_alive, members, voxel_count).reshape(-1)
    slot_of = (
        jnp.zeros((voxel_count,), jnp.int32)
        .at[flat_slots]
        .set(jnp.arange(windows_n * WIN, dtype=jnp.int32), mode="drop")
    )

    def to_voxels(slot_vals):
        return gather_rows(slot_vals.reshape(windows_n * WIN, -1), slot_of)

    win_all = gather_rows(table, members)
    kv_win = win_all[..., 2 * col_width :]
    received = padded(border_rows(kv_win, border), (("space", 0),), border)
    kv_ext = extend_windows(kv_win, received, border)

    key_index = jnp.concatenate(
        [border + jnp.arange(windows_n, dtype=jnp.int32)[:, None], neighbours], axis=1
    ).reshape(-1)
    dq_out, grad_ext = window_attention(key_index, length_ext, win_all, kv_ext)
    received_grads = padded(
        border_rows(grad_ext, border).astype(jnp.bfloat16), (("space", 0),), border
    ).astype(jnp.float32)
    own_grads = grad_ext[border : border + windows_n]
    own_grads = own_grads.at[:border].add(received_grads[:border])
    own_grads = own_grads.at[windows_n - border :].add(received_grads[3 * border :])
    slot_vals = jnp.concatenate(
        [dq_out, own_grads.astype(jnp.bfloat16)], axis=-1
    )
    vox = to_voxels(slot_vals).reshape(seq_n, rows, 4 * col_width)
    back = lax.all_to_all(vox, "seq", split_axis=0, concat_axis=0, tiled=True)
    back = back.reshape(seq_n, rows, 4, col_width)
    results = [
        jnp.transpose(back[:, :, i], (1, 0, 2)).reshape(rows, seq_n * col_width) for i in range(4)
    ]
    return (results[1], results[0], results[2], results[3])


def solution(mesh):
    in_specs = (
        P(("space", "seq"), None),
        P(("space", "seq"), None),
        P(("space", "seq"), None),
        P(("space", "seq"), None),
        P(),
        P("space", None),
        P("space", None),
    )
    out_specs = (
        P(("space", "seq"), None),
        P(("space", "seq"), None),
        P(("space", "seq"), None),
        P(("space", "seq"), None),
    )
    return jax.shard_map(shards, mesh=mesh, in_specs=in_specs, out_specs=out_specs, check_vma=False)
```

```python
import jax
import jax.numpy as jnp
from jax import lax
from jax.experimental import pallas as pl
from jax.experimental.pallas import tpu as pltpu
from jax.sharding import PartitionSpec as P

HEAD = 64
WIN = 64


MASKED_SCORE = -1e30


def padded(value, sides, width):
    for axis, dim in sides:
        count, length = (lax.axis_size(axis), value.shape[dim])
        up = [(i, (i + 1) % count) for i in range(count - 1)]
        down = [(j, i) for i, j in up]
        last = lax.slice_in_dim(value, length - width, length, axis=dim)
        first = lax.slice_in_dim(value, 0, width, axis=dim)
        before = lax.ppermute(last, axis, up)
        after = lax.ppermute(first, axis, down)
        value = jnp.concatenate([before, value, after], axis=dim)
    return value


def gather_rows(source, indices):
    return source.at[indices].get(mode="promise_in_bounds")


def to_windows(query_part, key_part, value_part, members):
    query_win = gather_rows(query_part, members)
    kv_win = gather_rows(jnp.concatenate([key_part, value_part], axis=1), members)
    return (query_win, kv_win)


def border_rows(source, border):
    return jnp.concatenate([source[:border], source[source.shape[0] - border :]], axis=0)


def extend_windows(kv_win, received, border):
    return jnp.concatenate([received[:border], kv_win, received[3 * border :]], axis=0)


def window_keys(block_id, per_block, border, neighbours):
    start_row = block_id * per_block
    own_rows = border + start_row + jnp.arange(per_block, dtype=jnp.int32)
    near_rows = lax.dynamic_slice_in_dim(neighbours, start_row, per_block, 0)
    return jnp.concatenate([own_rows[:, None], near_rows], axis=1)


def block_attention(query_blk, key_index, kv_ext, length_ext, head_count):
    block_n = query_blk.shape[0]
    col_width = query_blk.shape[-1]
    head_size = col_width // head_count
    key_rows = gather_rows(kv_ext, key_index).reshape(block_n, -1, 2 * col_width)
    key_length = gather_rows(length_ext, key_index)
    key_alive = (jnp.arange(WIN, dtype=jnp.int32)[None, None, :] < key_length[:, :, None]).reshape(
        block_n, -1
    )
    query_heads = query_blk.reshape(block_n, WIN, head_count, head_size)
    key_heads = key_rows[:, :, :col_width].reshape(block_n, -1, head_count, head_size)
    value_heads = key_rows[:, :, col_width:].reshape(block_n, -1, head_count, head_size)
    score_scale = head_size ** (-0.5)
    scores = (
        jnp.einsum("wqhd,wkhd->whqk", query_heads, key_heads, preferred_element_type=jnp.float32)
        * score_scale
    )
    scores = jnp.where(key_alive[:, None, None, :], scores, MASKED_SCORE)
    row_max = jnp.max(scores, axis=-1, keepdims=True)
    exp_scores = jnp.exp(scores - row_max)
    attn_probs = exp_scores / jnp.sum(exp_scores, axis=-1, keepdims=True)
    return (attn_probs, query_heads, key_heads, value_heads, score_scale)


def attention_kernel(idx_ref, len_ref, win_ref, kv_ref, out_ref, dkv_ref):
    windows_n = win_ref.shape[0]
    lanes = kv_ref.shape[-1]
    width = lanes // 2
    nb = idx_ref.shape[0] // windows_n
    keys = nb * WIN
    scale = HEAD ** (-0.5)
    dkv_ref[...] = jnp.zeros(dkv_ref.shape, dkv_ref.dtype)
    col = lax.broadcasted_iota(jnp.int32, (1, keys), 1)
    col_block = col // WIN
    col_slot = col % WIN
    lane = lax.broadcasted_iota(jnp.int32, (1, lanes), 1)
    first_half = lane < width
    slot_row = lax.broadcasted_iota(jnp.int32, (WIN, 1), 0)
    nt = (((1,), (1,)), ((), ()))
    tn = (((0,), (0,)), ((), ()))

    def body(w, carry):
        ids = [idx_ref[w * nb + j] for j in range(nb)]
        qg = win_ref[w, :, :lanes]
        zero = jnp.zeros_like(qg)
        q_pad = jnp.where(first_half, qg, zero)
        g_live = jnp.logical_and(jnp.logical_not(first_half), slot_row < len_ref[ids[0]])
        g_pad = jnp.where(g_live, qg, zero)
        qg_blocks = jnp.concatenate([q_pad, g_pad], axis=0)
        kv_all = jnp.concatenate([kv_ref[i] for i in ids], axis=0)
        limit = jnp.zeros((1, keys), jnp.int32)
        for j in range(nb):
            limit = jnp.where(col_block == j, len_ref[ids[j]], limit)
        alive = col_slot < limit
        both = lax.dot_general(qg_blocks, kv_all, nt, preferred_element_type=jnp.float32)
        scores = both[:WIN] * scale
        grad_probs = both[WIN:]
        scores = jnp.where(alive, scores, MASKED_SCORE)
        row_max = jnp.max(scores, axis=-1, keepdims=True)
        exp_scores = jnp.exp(scores - row_max)
        probs = exp_scores / jnp.sum(exp_scores, axis=-1, keepdims=True)
        weights = probs.astype(jnp.bfloat16)
        out_full = jnp.dot(weights, kv_all, preferred_element_type=jnp.float32).astype(jnp.bfloat16)
        delta = jnp.sum(
            g_pad.astype(jnp.float32) * out_full.astype(jnp.float32), axis=-1, keepdims=True
        )
        grad_scores = (probs * (grad_probs - delta) * scale).astype(jnp.bfloat16)
        dq_full = jnp.dot(grad_scores, kv_all, preferred_element_type=jnp.float32).astype(jnp.bfloat16)
        out_ref[w] = jnp.where(first_half, dq_full, out_full)
        score_blocks = jnp.concatenate([grad_scores, weights], axis=0)
        grad_kv = lax.dot_general(score_blocks, qg_blocks, tn, preferred_element_type=jnp.float32)
        for j in range(nb):
            dkv_ref[ids[j]] += grad_kv[j * WIN : (j + 1) * WIN]
        return carry

    lax.fori_loop(0, windows_n, body, 0, unroll=8)


def window_attention(key_index, length_ext, win_all, kv_ext):
    windows_n = win_all.shape[0]
    lanes = kv_ext.shape[-1]
    ext_n = kv_ext.shape[0]
    keys = (key_index.shape[0] // windows_n) * WIN
    flops = 2 * windows_n * WIN * keys * lanes * 6
    vmem = pl.BlockSpec(memory_space=pltpu.VMEM)
    smem = pl.BlockSpec(memory_space=pltpu.SMEM)
    return pl.pallas_call(
        attention_kernel,
        out_shape=(
            jax.ShapeDtypeStruct((windows_n, WIN, lanes), jnp.bfloat16),
            jax.ShapeDtypeStruct((ext_n, WIN, lanes), jnp.float32),
        ),
        in_specs=[smem, smem, vmem, vmem],
        out_specs=(vmem, vmem),
        compiler_params=pltpu.CompilerParams(vmem_limit_bytes=48 * 1024 * 1024),
        cost_estimate=pl.CostEstimate(
            flops=flops, transcendentals=windows_n * WIN * keys, bytes_accessed=8 * 1024 * 1024
        ),
    )(key_index, length_ext, win_all, kv_ext)


def shards(query_feats, key_feats, value_feats, grad_output, lengths, members, neighbours):
    group_idx = lax.axis_index("space")
    groups = lax.axis_size("space")
    windows_n = members.shape[0]
    border = windows_n // 6
    per_block = 8
    block_count = windows_n // per_block
    col_width = query_feats.shape[1] // lax.axis_size("seq")
    head_count = col_width // HEAD
    own_length = lax.dynamic_index_in_dim(lengths, group_idx, 0, keepdims=False)
    before_length = lax.dynamic_index_in_dim(
        lengths, jnp.maximum(group_idx - 1, 0), 0, keepdims=False
    )
    after_length = lax.dynamic_index_in_dim(
        lengths, jnp.minimum(group_idx + 1, groups - 1), 0, keepdims=False
    )
    length_ext = jnp.concatenate(
        [
            jnp.where(group_idx > 0, before_length[windows_n - border :], 0),
            own_length,
            jnp.where(group_idx < groups - 1, after_length[:border], 0),
        ]
    )
    slot_alive = jnp.arange(WIN, dtype=jnp.int32)[None, :] < own_length[:, None]
    rows = query_feats.shape[0]
    seq_n = lax.axis_size("seq")
    stacked = jnp.stack(
        [
            jnp.transpose(part.reshape(rows, seq_n, col_width), (1, 0, 2))
            for part in (query_feats, grad_output, key_feats, value_feats)
        ],
        axis=2,
    ).reshape(seq_n, rows, 4 * col_width)
    heads_all = lax.all_to_all(stacked, "seq", split_axis=0, concat_axis=0, tiled=True)
    voxel_count = seq_n * rows
    table = heads_all.reshape(voxel_count, 4 * col_width)
    flat_slots = jnp.where(slot_alive, members, voxel_count).reshape(-1)
    slot_of = (
        jnp.zeros((voxel_count,), jnp.int32)
        .at[flat_slots]
        .set(jnp.arange(windows_n * WIN, dtype=jnp.int32), mode="drop")
    )

    table, slot_of = lax.optimization_barrier((table, slot_of))

    def to_voxels(slot_vals):
        return gather_rows(slot_vals.reshape(windows_n * WIN, -1), slot_of)

    win_all = gather_rows(table, members)
    kv_win = win_all[..., 2 * col_width :]
    received = padded(border_rows(kv_win, border), (("space", 0),), border)
    kv_ext = extend_windows(kv_win, received, border)

    key_index = jnp.concatenate(
        [border + jnp.arange(windows_n, dtype=jnp.int32)[:, None], neighbours], axis=1
    ).reshape(-1)
    dq_out, grad_ext = window_attention(key_index, length_ext, win_all, kv_ext)
    received_grads = padded(
        border_rows(grad_ext, border).astype(jnp.bfloat16), (("space", 0),), border
    ).astype(jnp.float32)
    own_grads = grad_ext[border : border + windows_n]
    own_grads = own_grads.at[:border].add(received_grads[:border])
    own_grads = own_grads.at[windows_n - border :].add(received_grads[3 * border :])
    slot_vals = jnp.concatenate(
        [dq_out, own_grads.astype(jnp.bfloat16)], axis=-1
    )
    vox = to_voxels(slot_vals).reshape(seq_n, rows, 4 * col_width)
    back = lax.all_to_all(vox, "seq", split_axis=0, concat_axis=0, tiled=True)
    back = back.reshape(seq_n, rows, 4, col_width)
    results = [
        jnp.transpose(back[:, :, i], (1, 0, 2)).reshape(rows, seq_n * col_width) for i in range(4)
    ]
    return (results[1], results[0], results[2], results[3])


def solution(mesh):
    in_specs = (
        P(("space", "seq"), None),
        P(("space", "seq"), None),
        P(("space", "seq"), None),
        P(("space", "seq"), None),
        P(),
        P("space", None),
        P("space", None),
    )
    out_specs = (
        P(("space", "seq"), None),
        P(("space", "seq"), None),
        P(("space", "seq"), None),
        P(("space", "seq"), None),
    )
    return jax.shard_map(shards, mesh=mesh, in_specs=in_specs, out_specs=out_specs, check_vma=False)
```

```python
import jax
import jax.numpy as jnp
from jax import lax
from jax.experimental import pallas as pl
from jax.experimental.pallas import tpu as pltpu
from jax.sharding import PartitionSpec as P

HEAD = 64
WIN = 64


MASKED_SCORE = -1e30


def padded(value, sides, width):
    for axis, dim in sides:
        count, length = (lax.axis_size(axis), value.shape[dim])
        up = [(i, (i + 1) % count) for i in range(count - 1)]
        down = [(j, i) for i, j in up]
        last = lax.slice_in_dim(value, length - width, length, axis=dim)
        first = lax.slice_in_dim(value, 0, width, axis=dim)
        before = lax.ppermute(last, axis, up)
        after = lax.ppermute(first, axis, down)
        value = jnp.concatenate([before, value, after], axis=dim)
    return value


def gather_rows(source, indices):
    return source.at[indices].get(mode="promise_in_bounds")


def to_windows(query_part, key_part, value_part, members):
    query_win = gather_rows(query_part, members)
    kv_win = gather_rows(jnp.concatenate([key_part, value_part], axis=1), members)
    return (query_win, kv_win)


def border_rows(source, border):
    return jnp.concatenate([source[:border], source[source.shape[0] - border :]], axis=0)


def extend_windows(kv_win, received, border):
    return jnp.concatenate([received[:border], kv_win, received[3 * border :]], axis=0)


def window_keys(block_id, per_block, border, neighbours):
    start_row = block_id * per_block
    own_rows = border + start_row + jnp.arange(per_block, dtype=jnp.int32)
    near_rows = lax.dynamic_slice_in_dim(neighbours, start_row, per_block, 0)
    return jnp.concatenate([own_rows[:, None], near_rows], axis=1)


def block_attention(query_blk, key_index, kv_ext, length_ext, head_count):
    block_n = query_blk.shape[0]
    col_width = query_blk.shape[-1]
    head_size = col_width // head_count
    key_rows = gather_rows(kv_ext, key_index).reshape(block_n, -1, 2 * col_width)
    key_length = gather_rows(length_ext, key_index)
    key_alive = (jnp.arange(WIN, dtype=jnp.int32)[None, None, :] < key_length[:, :, None]).reshape(
        block_n, -1
    )
    query_heads = query_blk.reshape(block_n, WIN, head_count, head_size)
    key_heads = key_rows[:, :, :col_width].reshape(block_n, -1, head_count, head_size)
    value_heads = key_rows[:, :, col_width:].reshape(block_n, -1, head_count, head_size)
    score_scale = head_size ** (-0.5)
    scores = (
        jnp.einsum("wqhd,wkhd->whqk", query_heads, key_heads, preferred_element_type=jnp.float32)
        * score_scale
    )
    scores = jnp.where(key_alive[:, None, None, :], scores, MASKED_SCORE)
    row_max = jnp.max(scores, axis=-1, keepdims=True)
    exp_scores = jnp.exp(scores - row_max)
    attn_probs = exp_scores / jnp.sum(exp_scores, axis=-1, keepdims=True)
    return (attn_probs, query_heads, key_heads, value_heads, score_scale)


def attention_kernel(idx_ref, len_ref, win_ref, kv_ref, out_ref, dkv_ref, rim_ref):
    windows_n = win_ref.shape[0]
    lanes = kv_ref.shape[-1]
    width = lanes // 2
    nb = idx_ref.shape[0] // windows_n
    keys = nb * WIN
    scale = HEAD ** (-0.5)
    dkv_ref[...] = jnp.zeros(dkv_ref.shape, dkv_ref.dtype)
    col = lax.broadcasted_iota(jnp.int32, (1, keys), 1)
    col_block = col // WIN
    col_slot = col % WIN
    lane = lax.broadcasted_iota(jnp.int32, (1, lanes), 1)
    first_half = lane < width
    slot_row = lax.broadcasted_iota(jnp.int32, (WIN, 1), 0)
    nt = (((1,), (1,)), ((), ()))
    tn = (((0,), (0,)), ((), ()))

    def body(w, carry):
        ids = [idx_ref[w * nb + j] for j in range(nb)]
        qg = win_ref[w, :, :lanes]
        zero = jnp.zeros_like(qg)
        q_pad = jnp.where(first_half, qg, zero)
        g_live = jnp.logical_and(jnp.logical_not(first_half), slot_row < len_ref[ids[0]])
        g_pad = jnp.where(g_live, qg, zero)
        qg_blocks = jnp.concatenate([q_pad, g_pad], axis=0)
        kv_all = jnp.concatenate([kv_ref[i] for i in ids], axis=0)
        limit = jnp.zeros((1, keys), jnp.int32)
        for j in range(nb):
            limit = jnp.where(col_block == j, len_ref[ids[j]], limit)
        alive = col_slot < limit
        both = lax.dot_general(qg_blocks, kv_all, nt, preferred_element_type=jnp.float32)
        scores = both[:WIN] * scale
        grad_probs = both[WIN:]
        scores = jnp.where(alive, scores, MASKED_SCORE)
        row_max = jnp.max(scores, axis=-1, keepdims=True)
        exp_scores = jnp.exp(scores - row_max)
        probs = exp_scores / jnp.sum(exp_scores, axis=-1, keepdims=True)
        weights = probs.astype(jnp.bfloat16)
        out_full = jnp.dot(weights, kv_all, preferred_element_type=jnp.float32).astype(jnp.bfloat16)
        delta = jnp.sum(
            g_pad.astype(jnp.float32) * out_full.astype(jnp.float32), axis=-1, keepdims=True
        )
        grad_scores = (probs * (grad_probs - delta) * scale).astype(jnp.bfloat16)
        dq_full = jnp.dot(grad_scores, kv_all, preferred_element_type=jnp.float32).astype(jnp.bfloat16)
        out_ref[w] = jnp.where(first_half, dq_full, out_full)
        score_blocks = jnp.concatenate([grad_scores, weights], axis=0)
        grad_kv = lax.dot_general(score_blocks, qg_blocks, tn, preferred_element_type=jnp.float32)
        for j in range(nb):
            dkv_ref[ids[j]] += grad_kv[j * WIN : (j + 1) * WIN]
        return carry

    lax.fori_loop(0, windows_n, body, 0, unroll=8)
    ext_n = dkv_ref.shape[0]
    border = rim_ref.shape[0] // 2
    rim_ref[:border] = dkv_ref[:border].astype(rim_ref.dtype)
    rim_ref[border:] = dkv_ref[ext_n - border :].astype(rim_ref.dtype)


def window_attention(key_index, length_ext, win_all, kv_ext):
    windows_n = win_all.shape[0]
    lanes = kv_ext.shape[-1]
    ext_n = kv_ext.shape[0]
    keys = (key_index.shape[0] // windows_n) * WIN
    flops = 2 * windows_n * WIN * keys * lanes * 6
    vmem = pl.BlockSpec(memory_space=pltpu.VMEM)
    smem = pl.BlockSpec(memory_space=pltpu.SMEM)
    return pl.pallas_call(
        attention_kernel,
        out_shape=(
            jax.ShapeDtypeStruct((windows_n, WIN, lanes), jnp.bfloat16),
            jax.ShapeDtypeStruct((ext_n, WIN, lanes), jnp.float32),
            jax.ShapeDtypeStruct((ext_n - windows_n, WIN, lanes), jnp.bfloat16),
        ),
        in_specs=[smem, smem, vmem, vmem],
        out_specs=(vmem, vmem, vmem),
        compiler_params=pltpu.CompilerParams(vmem_limit_bytes=48 * 1024 * 1024),
        cost_estimate=pl.CostEstimate(
            flops=flops, transcendentals=windows_n * WIN * keys, bytes_accessed=8 * 1024 * 1024
        ),
    )(key_index, length_ext, win_all, kv_ext)


def shards(query_feats, key_feats, value_feats, grad_output, lengths, members, neighbours):
    group_idx = lax.axis_index("space")
    groups = lax.axis_size("space")
    windows_n = members.shape[0]
    border = windows_n // 6
    per_block = 8
    block_count = windows_n // per_block
    col_width = query_feats.shape[1] // lax.axis_size("seq")
    head_count = col_width // HEAD
    own_length = lax.dynamic_index_in_dim(lengths, group_idx, 0, keepdims=False)
    before_length = lax.dynamic_index_in_dim(
        lengths, jnp.maximum(group_idx - 1, 0), 0, keepdims=False
    )
    after_length = lax.dynamic_index_in_dim(
        lengths, jnp.minimum(group_idx + 1, groups - 1), 0, keepdims=False
    )
    length_ext = jnp.concatenate(
        [
            jnp.where(group_idx > 0, before_length[windows_n - border :], 0),
            own_length,
            jnp.where(group_idx < groups - 1, after_length[:border], 0),
        ]
    )
    slot_alive = jnp.arange(WIN, dtype=jnp.int32)[None, :] < own_length[:, None]
    rows = query_feats.shape[0]
    seq_n = lax.axis_size("seq")
    stacked = jnp.stack(
        [
            jnp.transpose(part.reshape(rows, seq_n, col_width), (1, 0, 2))
            for part in (query_feats, grad_output, key_feats, value_feats)
        ],
        axis=2,
    ).reshape(seq_n, rows, 4 * col_width)
    heads_all = lax.all_to_all(stacked, "seq", split_axis=0, concat_axis=0, tiled=True)
    voxel_count = seq_n * rows
    table = heads_all.reshape(voxel_count, 4 * col_width)
    flat_slots = jnp.where(slot_alive, members, voxel_count).reshape(-1)
    slot_of = (
        jnp.zeros((voxel_count,), jnp.int32)
        .at[flat_slots]
        .set(jnp.arange(windows_n * WIN, dtype=jnp.int32), mode="drop")
    )

    table, slot_of = lax.optimization_barrier((table, slot_of))

    def to_voxels(slot_vals):
        return gather_rows(slot_vals.reshape(windows_n * WIN, -1), slot_of)

    win_all = gather_rows(table, members)
    kv_win = win_all[..., 2 * col_width :]
    received = padded(border_rows(kv_win, border), (("space", 0),), border)
    kv_ext = extend_windows(kv_win, received, border)

    key_index = jnp.concatenate(
        [border + jnp.arange(windows_n, dtype=jnp.int32)[:, None], neighbours], axis=1
    ).reshape(-1)
    dq_out, grad_ext, rim_grads = window_attention(key_index, length_ext, win_all, kv_ext)
    received_grads = padded(rim_grads, (("space", 0),), border).astype(jnp.float32)
    own_grads = grad_ext[border : border + windows_n]
    own_grads = own_grads.at[:border].add(received_grads[:border])
    own_grads = own_grads.at[windows_n - border :].add(received_grads[3 * border :])
    slot_vals = jnp.concatenate(
        [dq_out, own_grads.astype(jnp.bfloat16)], axis=-1
    )
    vox = to_voxels(slot_vals).reshape(seq_n, rows, 4 * col_width)
    back = lax.all_to_all(vox, "seq", split_axis=0, concat_axis=0, tiled=True)
    back = back.reshape(seq_n, rows, 4, col_width)
    results = [
        jnp.transpose(back[:, :, i], (1, 0, 2)).reshape(rows, seq_n * col_width) for i in range(4)
    ]
    return (results[1], results[0], results[2], results[3])


def solution(mesh):
    in_specs = (
        P(("space", "seq"), None),
        P(("space", "seq"), None),
        P(("space", "seq"), None),
        P(("space", "seq"), None),
        P(),
        P("space", None),
        P("space", None),
    )
    out_specs = (
        P(("space", "seq"), None),
        P(("space", "seq"), None),
        P(("space", "seq"), None),
        P(("space", "seq"), None),
    )
    return jax.shard_map(shards, mesh=mesh, in_specs=in_specs, out_specs=out_specs, check_vma=False)
```

```python
import jax
import jax.numpy as jnp
from jax import lax
from jax.experimental import pallas as pl
from jax.experimental.pallas import tpu as pltpu
from jax.sharding import PartitionSpec as P

HEAD = 64
WIN = 64


MASKED_SCORE = -1e30


def padded(value, sides, width):
    for axis, dim in sides:
        count, length = (lax.axis_size(axis), value.shape[dim])
        up = [(i, (i + 1) % count) for i in range(count - 1)]
        down = [(j, i) for i, j in up]
        last = lax.slice_in_dim(value, length - width, length, axis=dim)
        first = lax.slice_in_dim(value, 0, width, axis=dim)
        before = lax.ppermute(last, axis, up)
        after = lax.ppermute(first, axis, down)
        value = jnp.concatenate([before, value, after], axis=dim)
    return value


def gather_rows(source, indices):
    return source.at[indices].get(mode="promise_in_bounds")


def to_windows(query_part, key_part, value_part, members):
    query_win = gather_rows(query_part, members)
    kv_win = gather_rows(jnp.concatenate([key_part, value_part], axis=1), members)
    return (query_win, kv_win)


def border_rows(source, border):
    return jnp.concatenate([source[:border], source[source.shape[0] - border :]], axis=0)


def extend_windows(kv_win, received, border):
    return jnp.concatenate([received[:border], kv_win, received[3 * border :]], axis=0)


def window_keys(block_id, per_block, border, neighbours):
    start_row = block_id * per_block
    own_rows = border + start_row + jnp.arange(per_block, dtype=jnp.int32)
    near_rows = lax.dynamic_slice_in_dim(neighbours, start_row, per_block, 0)
    return jnp.concatenate([own_rows[:, None], near_rows], axis=1)


def block_attention(query_blk, key_index, kv_ext, length_ext, head_count):
    block_n = query_blk.shape[0]
    col_width = query_blk.shape[-1]
    head_size = col_width // head_count
    key_rows = gather_rows(kv_ext, key_index).reshape(block_n, -1, 2 * col_width)
    key_length = gather_rows(length_ext, key_index)
    key_alive = (jnp.arange(WIN, dtype=jnp.int32)[None, None, :] < key_length[:, :, None]).reshape(
        block_n, -1
    )
    query_heads = query_blk.reshape(block_n, WIN, head_count, head_size)
    key_heads = key_rows[:, :, :col_width].reshape(block_n, -1, head_count, head_size)
    value_heads = key_rows[:, :, col_width:].reshape(block_n, -1, head_count, head_size)
    score_scale = head_size ** (-0.5)
    scores = (
        jnp.einsum("wqhd,wkhd->whqk", query_heads, key_heads, preferred_element_type=jnp.float32)
        * score_scale
    )
    scores = jnp.where(key_alive[:, None, None, :], scores, MASKED_SCORE)
    row_max = jnp.max(scores, axis=-1, keepdims=True)
    exp_scores = jnp.exp(scores - row_max)
    attn_probs = exp_scores / jnp.sum(exp_scores, axis=-1, keepdims=True)
    return (attn_probs, query_heads, key_heads, value_heads, score_scale)


def attention_kernel(idx_ref, len_ref, win_ref, kv_ref, out_ref, dkv_ref, rim_ref):
    windows_n = win_ref.shape[0]
    lanes = kv_ref.shape[-1]
    width = lanes // 2
    nb = idx_ref.shape[0] // windows_n
    keys = nb * WIN
    scale = HEAD ** (-0.5)
    dkv_ref[...] = jnp.zeros(dkv_ref.shape, dkv_ref.dtype)
    col = lax.broadcasted_iota(jnp.int32, (1, keys), 1)
    col_block = col // WIN
    col_slot = col % WIN
    lane = lax.broadcasted_iota(jnp.int32, (1, lanes), 1)
    first_half = lane < width
    slot_row = lax.broadcasted_iota(jnp.int32, (WIN, 1), 0)
    nt = (((1,), (1,)), ((), ()))
    tn = (((0,), (0,)), ((), ()))

    def body(w, carry):
        ids = [idx_ref[w * nb + j] for j in range(nb)]
        qg = win_ref[w, :, :lanes]
        zero = jnp.zeros_like(qg)
        q_pad = jnp.where(first_half, qg, zero)
        g_live = jnp.logical_and(jnp.logical_not(first_half), slot_row < len_ref[ids[0]])
        g_pad = jnp.where(g_live, qg, zero)
        qg_blocks = jnp.concatenate([q_pad, g_pad], axis=0)
        kv_all = jnp.concatenate([kv_ref[i] for i in ids], axis=0)
        limit = jnp.zeros((1, keys), jnp.int32)
        for j in range(nb):
            limit = jnp.where(col_block == j, len_ref[ids[j]], limit)
        alive = col_slot < limit
        both = lax.dot_general(qg_blocks, kv_all, nt, preferred_element_type=jnp.float32)
        scores = both[:WIN] * scale
        grad_probs = both[WIN:]
        scores = jnp.where(alive, scores, MASKED_SCORE)
        row_max = jnp.max(scores, axis=-1, keepdims=True)
        exp_scores = jnp.exp(scores - row_max)
        probs = exp_scores / jnp.sum(exp_scores, axis=-1, keepdims=True)
        weights = probs.astype(jnp.bfloat16)
        out_full = jnp.dot(weights, kv_all, preferred_element_type=jnp.float32).astype(jnp.bfloat16)
        delta = jnp.sum(
            g_pad.astype(jnp.float32) * out_full.astype(jnp.float32), axis=-1, keepdims=True
        )
        grad_scores = (probs * (grad_probs - delta) * scale).astype(jnp.bfloat16)
        dq_full = jnp.dot(grad_scores, kv_all, preferred_element_type=jnp.float32).astype(jnp.bfloat16)
        out_ref[w] = jnp.where(first_half, dq_full, out_full)
        score_blocks = jnp.concatenate([grad_scores, weights], axis=0)
        grad_kv = lax.dot_general(score_blocks, qg_blocks, tn, preferred_element_type=jnp.float32)
        for j in range(nb):
            dkv_ref[ids[j]] += grad_kv[j * WIN : (j + 1) * WIN]
        return carry

    lax.fori_loop(0, windows_n, body, 0, unroll=16)
    ext_n = dkv_ref.shape[0]
    border = rim_ref.shape[0] // 2
    rim_ref[:border] = dkv_ref[:border].astype(rim_ref.dtype)
    rim_ref[border:] = dkv_ref[ext_n - border :].astype(rim_ref.dtype)


def window_attention(key_index, length_ext, win_all, kv_ext):
    windows_n = win_all.shape[0]
    lanes = kv_ext.shape[-1]
    ext_n = kv_ext.shape[0]
    keys = (key_index.shape[0] // windows_n) * WIN
    flops = 2 * windows_n * WIN * keys * lanes * 6
    vmem = pl.BlockSpec(memory_space=pltpu.VMEM)
    smem = pl.BlockSpec(memory_space=pltpu.SMEM)
    return pl.pallas_call(
        attention_kernel,
        out_shape=(
            jax.ShapeDtypeStruct((windows_n, WIN, lanes), jnp.bfloat16),
            jax.ShapeDtypeStruct((ext_n, WIN, lanes), jnp.float32),
            jax.ShapeDtypeStruct((ext_n - windows_n, WIN, lanes), jnp.bfloat16),
        ),
        in_specs=[smem, smem, vmem, vmem],
        out_specs=(vmem, vmem, vmem),
        compiler_params=pltpu.CompilerParams(vmem_limit_bytes=48 * 1024 * 1024),
        cost_estimate=pl.CostEstimate(
            flops=flops, transcendentals=windows_n * WIN * keys, bytes_accessed=8 * 1024 * 1024
        ),
    )(key_index, length_ext, win_all, kv_ext)


def shards(query_feats, key_feats, value_feats, grad_output, lengths, members, neighbours):
    group_idx = lax.axis_index("space")
    groups = lax.axis_size("space")
    windows_n = members.shape[0]
    border = windows_n // 6
    per_block = 8
    block_count = windows_n // per_block
    col_width = query_feats.shape[1] // lax.axis_size("seq")
    head_count = col_width // HEAD
    own_length = lax.dynamic_index_in_dim(lengths, group_idx, 0, keepdims=False)
    before_length = lax.dynamic_index_in_dim(
        lengths, jnp.maximum(group_idx - 1, 0), 0, keepdims=False
    )
    after_length = lax.dynamic_index_in_dim(
        lengths, jnp.minimum(group_idx + 1, groups - 1), 0, keepdims=False
    )
    length_ext = jnp.concatenate(
        [
            jnp.where(group_idx > 0, before_length[windows_n - border :], 0),
            own_length,
            jnp.where(group_idx < groups - 1, after_length[:border], 0),
        ]
    )
    slot_alive = jnp.arange(WIN, dtype=jnp.int32)[None, :] < own_length[:, None]
    rows = query_feats.shape[0]
    seq_n = lax.axis_size("seq")
    stacked = jnp.stack(
        [
            jnp.transpose(part.reshape(rows, seq_n, col_width), (1, 0, 2))
            for part in (query_feats, grad_output, key_feats, value_feats)
        ],
        axis=2,
    ).reshape(seq_n, rows, 4 * col_width)
    heads_all = lax.all_to_all(stacked, "seq", split_axis=0, concat_axis=0, tiled=True)
    voxel_count = seq_n * rows
    table = heads_all.reshape(voxel_count, 4 * col_width)
    flat_slots = jnp.where(slot_alive, members, voxel_count).reshape(-1)
    slot_of = (
        jnp.zeros((voxel_count,), jnp.int32)
        .at[flat_slots]
        .set(jnp.arange(windows_n * WIN, dtype=jnp.int32), mode="drop")
    )

    table, slot_of = lax.optimization_barrier((table, slot_of))

    def to_voxels(slot_vals):
        return gather_rows(slot_vals.reshape(windows_n * WIN, -1), slot_of)

    win_all = gather_rows(table, members)
    kv_win = win_all[..., 2 * col_width :]
    received = padded(border_rows(kv_win, border), (("space", 0),), border)
    kv_ext = extend_windows(kv_win, received, border)

    key_index = jnp.concatenate(
        [border + jnp.arange(windows_n, dtype=jnp.int32)[:, None], neighbours], axis=1
    ).reshape(-1)
    dq_out, grad_ext, rim_grads = window_attention(key_index, length_ext, win_all, kv_ext)
    received_grads = padded(rim_grads, (("space", 0),), border).astype(jnp.float32)
    own_grads = grad_ext[border : border + windows_n]
    own_grads = own_grads.at[:border].add(received_grads[:border])
    own_grads = own_grads.at[windows_n - border :].add(received_grads[3 * border :])
    slot_vals = jnp.concatenate(
        [dq_out, own_grads.astype(jnp.bfloat16)], axis=-1
    )
    vox = to_voxels(slot_vals).reshape(seq_n, rows, 4 * col_width)
    back = lax.all_to_all(vox, "seq", split_axis=0, concat_axis=0, tiled=True)
    back = back.reshape(seq_n, rows, 4, col_width)
    results = [
        jnp.transpose(back[:, :, i], (1, 0, 2)).reshape(rows, seq_n * col_width) for i in range(4)
    ]
    return (results[1], results[0], results[2], results[3])


def solution(mesh):
    in_specs = (
        P(("space", "seq"), None),
        P(("space", "seq"), None),
        P(("space", "seq"), None),
        P(("space", "seq"), None),
        P(),
        P("space", None),
        P("space", None),
    )
    out_specs = (
        P(("space", "seq"), None),
        P(("space", "seq"), None),
        P(("space", "seq"), None),
        P(("space", "seq"), None),
    )
    return jax.shard_map(shards, mesh=mesh, in_specs=in_specs, out_specs=out_specs, check_vma=False)
```

```python
import jax
import jax.numpy as jnp
from jax import lax
from jax.experimental import pallas as pl
from jax.experimental.pallas import tpu as pltpu
from jax.sharding import PartitionSpec as P

HEAD = 64
WIN = 64


MASKED_SCORE = -1e30


def padded(value, sides, width):
    for axis, dim in sides:
        count, length = (lax.axis_size(axis), value.shape[dim])
        up = [(i, (i + 1) % count) for i in range(count - 1)]
        down = [(j, i) for i, j in up]
        last = lax.slice_in_dim(value, length - width, length, axis=dim)
        first = lax.slice_in_dim(value, 0, width, axis=dim)
        before = lax.ppermute(last, axis, up)
        after = lax.ppermute(first, axis, down)
        value = jnp.concatenate([before, value, after], axis=dim)
    return value


def gather_rows(source, indices):
    return source.at[indices].get(mode="promise_in_bounds")


def to_windows(query_part, key_part, value_part, members):
    query_win = gather_rows(query_part, members)
    kv_win = gather_rows(jnp.concatenate([key_part, value_part], axis=1), members)
    return (query_win, kv_win)


def border_rows(source, border):
    return jnp.concatenate([source[:border], source[source.shape[0] - border :]], axis=0)


def extend_windows(kv_win, received, border):
    return jnp.concatenate([received[:border], kv_win, received[3 * border :]], axis=0)


def window_keys(block_id, per_block, border, neighbours):
    start_row = block_id * per_block
    own_rows = border + start_row + jnp.arange(per_block, dtype=jnp.int32)
    near_rows = lax.dynamic_slice_in_dim(neighbours, start_row, per_block, 0)
    return jnp.concatenate([own_rows[:, None], near_rows], axis=1)


def block_attention(query_blk, key_index, kv_ext, length_ext, head_count):
    block_n = query_blk.shape[0]
    col_width = query_blk.shape[-1]
    head_size = col_width // head_count
    key_rows = gather_rows(kv_ext, key_index).reshape(block_n, -1, 2 * col_width)
    key_length = gather_rows(length_ext, key_index)
    key_alive = (jnp.arange(WIN, dtype=jnp.int32)[None, None, :] < key_length[:, :, None]).reshape(
        block_n, -1
    )
    query_heads = query_blk.reshape(block_n, WIN, head_count, head_size)
    key_heads = key_rows[:, :, :col_width].reshape(block_n, -1, head_count, head_size)
    value_heads = key_rows[:, :, col_width:].reshape(block_n, -1, head_count, head_size)
    score_scale = head_size ** (-0.5)
    scores = (
        jnp.einsum("wqhd,wkhd->whqk", query_heads, key_heads, preferred_element_type=jnp.float32)
        * score_scale
    )
    scores = jnp.where(key_alive[:, None, None, :], scores, MASKED_SCORE)
    row_max = jnp.max(scores, axis=-1, keepdims=True)
    exp_scores = jnp.exp(scores - row_max)
    attn_probs = exp_scores / jnp.sum(exp_scores, axis=-1, keepdims=True)
    return (attn_probs, query_heads, key_heads, value_heads, score_scale)


def attention_kernel(idx_ref, len_ref, win_ref, kv_ref, out_ref, own_rim_ref, rim_ref, dkv_ref):
    windows_n = win_ref.shape[0]
    lanes = kv_ref.shape[-1]
    width = lanes // 2
    nb = idx_ref.shape[0] // windows_n
    keys = nb * WIN
    scale = HEAD ** (-0.5)
    dkv_ref[...] = jnp.zeros(dkv_ref.shape, dkv_ref.dtype)
    col = lax.broadcasted_iota(jnp.int32, (1, keys), 1)
    col_block = col // WIN
    col_slot = col % WIN
    lane = lax.broadcasted_iota(jnp.int32, (1, lanes), 1)
    first_half = lane < width
    slot_row = lax.broadcasted_iota(jnp.int32, (WIN, 1), 0)
    nt = (((1,), (1,)), ((), ()))
    tn = (((0,), (0,)), ((), ()))

    def body(w, carry):
        ids = [idx_ref[w * nb + j] for j in range(nb)]
        qg = win_ref[w, :, :lanes]
        zero = jnp.zeros_like(qg)
        q_pad = jnp.where(first_half, qg, zero)
        g_live = jnp.logical_and(jnp.logical_not(first_half), slot_row < len_ref[ids[0]])
        g_pad = jnp.where(g_live, qg, zero)
        qg_blocks = jnp.concatenate([q_pad, g_pad], axis=0)
        kv_all = jnp.concatenate([kv_ref[i] for i in ids], axis=0)
        limit = jnp.zeros((1, keys), jnp.int32)
        for j in range(nb):
            limit = jnp.where(col_block == j, len_ref[ids[j]], limit)
        alive = col_slot < limit
        both = lax.dot_general(qg_blocks, kv_all, nt, preferred_element_type=jnp.float32)
        scores = both[:WIN] * scale
        grad_probs = both[WIN:]
        scores = jnp.where(alive, scores, MASKED_SCORE)
        row_max = jnp.max(scores, axis=-1, keepdims=True)
        exp_scores = jnp.exp(scores - row_max)
        probs = exp_scores / jnp.sum(exp_scores, axis=-1, keepdims=True)
        weights = probs.astype(jnp.bfloat16)
        out_full = jnp.dot(weights, kv_all, preferred_element_type=jnp.float32).astype(jnp.bfloat16)
        delta = jnp.sum(
            g_pad.astype(jnp.float32) * out_full.astype(jnp.float32), axis=-1, keepdims=True
        )
        grad_scores = (probs * (grad_probs - delta) * scale).astype(jnp.bfloat16)
        dq_full = jnp.dot(grad_scores, kv_all, preferred_element_type=jnp.float32).astype(jnp.bfloat16)
        out_ref[w, :, :lanes] = jnp.where(first_half, dq_full, out_full)
        score_blocks = jnp.concatenate([grad_scores, weights], axis=0)
        grad_kv = lax.dot_general(score_blocks, qg_blocks, tn, preferred_element_type=jnp.float32)
        for j in range(nb):
            dkv_ref[ids[j]] += grad_kv[j * WIN : (j + 1) * WIN]
        return carry

    lax.fori_loop(0, windows_n, body, 0, unroll=16)
    ext_n = dkv_ref.shape[0]
    border = rim_ref.shape[0] // 2
    rim_ref[:border] = dkv_ref[:border].astype(rim_ref.dtype)
    rim_ref[border:] = dkv_ref[ext_n - border :].astype(rim_ref.dtype)
    own_rim_ref[:border] = dkv_ref[border : 2 * border]
    own_rim_ref[border:] = dkv_ref[ext_n - 2 * border : ext_n - border]
    out_ref[:, :, lanes:] = dkv_ref[border : border + windows_n].astype(out_ref.dtype)


def window_attention(key_index, length_ext, win_all, kv_ext):
    windows_n = win_all.shape[0]
    lanes = kv_ext.shape[-1]
    ext_n = kv_ext.shape[0]
    keys = (key_index.shape[0] // windows_n) * WIN
    flops = 2 * windows_n * WIN * keys * lanes * 6
    vmem = pl.BlockSpec(memory_space=pltpu.VMEM)
    smem = pl.BlockSpec(memory_space=pltpu.SMEM)
    return pl.pallas_call(
        attention_kernel,
        out_shape=(
            jax.ShapeDtypeStruct((windows_n, WIN, 2 * lanes), jnp.bfloat16),
            jax.ShapeDtypeStruct((ext_n - windows_n, WIN, lanes), jnp.float32),
            jax.ShapeDtypeStruct((ext_n - windows_n, WIN, lanes), jnp.bfloat16),
        ),
        in_specs=[smem, smem, vmem, vmem],
        out_specs=(vmem, vmem, vmem),
        scratch_shapes=[pltpu.VMEM((ext_n, WIN, lanes), jnp.float32)],
        compiler_params=pltpu.CompilerParams(vmem_limit_bytes=48 * 1024 * 1024),
        cost_estimate=pl.CostEstimate(
            flops=flops, transcendentals=windows_n * WIN * keys, bytes_accessed=8 * 1024 * 1024
        ),
    )(key_index, length_ext, win_all, kv_ext)


def shards(query_feats, key_feats, value_feats, grad_output, lengths, members, neighbours):
    group_idx = lax.axis_index("space")
    groups = lax.axis_size("space")
    windows_n = members.shape[0]
    border = windows_n // 6
    per_block = 8
    block_count = windows_n // per_block
    col_width = query_feats.shape[1] // lax.axis_size("seq")
    head_count = col_width // HEAD
    own_length = lax.dynamic_index_in_dim(lengths, group_idx, 0, keepdims=False)
    before_length = lax.dynamic_index_in_dim(
        lengths, jnp.maximum(group_idx - 1, 0), 0, keepdims=False
    )
    after_length = lax.dynamic_index_in_dim(
        lengths, jnp.minimum(group_idx + 1, groups - 1), 0, keepdims=False
    )
    length_ext = jnp.concatenate(
        [
            jnp.where(group_idx > 0, before_length[windows_n - border :], 0),
            own_length,
            jnp.where(group_idx < groups - 1, after_length[:border], 0),
        ]
    )
    slot_alive = jnp.arange(WIN, dtype=jnp.int32)[None, :] < own_length[:, None]
    rows = query_feats.shape[0]
    seq_n = lax.axis_size("seq")
    stacked = jnp.stack(
        [
            jnp.transpose(part.reshape(rows, seq_n, col_width), (1, 0, 2))
            for part in (query_feats, grad_output, key_feats, value_feats)
        ],
        axis=2,
    ).reshape(seq_n, rows, 4 * col_width)
    heads_all = lax.all_to_all(stacked, "seq", split_axis=0, concat_axis=0, tiled=True)
    voxel_count = seq_n * rows
    table = heads_all.reshape(voxel_count, 4 * col_width)
    flat_slots = jnp.where(slot_alive, members, voxel_count).reshape(-1)
    slot_of = (
        jnp.zeros((voxel_count,), jnp.int32)
        .at[flat_slots]
        .set(jnp.arange(windows_n * WIN, dtype=jnp.int32), mode="drop")
    )

    table, slot_of = lax.optimization_barrier((table, slot_of))

    def to_voxels(slot_vals):
        return gather_rows(slot_vals.reshape(windows_n * WIN, -1), slot_of)

    win_all = gather_rows(table, members)
    kv_win = win_all[..., 2 * col_width :]
    received = padded(border_rows(kv_win, border), (("space", 0),), border)
    kv_ext = extend_windows(kv_win, received, border)

    key_index = jnp.concatenate(
        [border + jnp.arange(windows_n, dtype=jnp.int32)[:, None], neighbours], axis=1
    ).reshape(-1)
    slot_vals, own_rim, rim_grads = window_attention(key_index, length_ext, win_all, kv_ext)
    received_grads = padded(rim_grads, (("space", 0),), border).astype(jnp.float32)
    low = (own_rim[:border] + received_grads[:border]).astype(jnp.bfloat16)
    high = (own_rim[border:] + received_grads[3 * border :]).astype(jnp.bfloat16)
    slot_vals = slot_vals.at[:border, :, 2 * col_width :].set(low)
    slot_vals = slot_vals.at[windows_n - border :, :, 2 * col_width :].set(high)
    vox = to_voxels(slot_vals).reshape(seq_n, rows, 4 * col_width)
    back = lax.all_to_all(vox, "seq", split_axis=0, concat_axis=0, tiled=True)
    back = back.reshape(seq_n, rows, 4, col_width)
    results = [
        jnp.transpose(back[:, :, i], (1, 0, 2)).reshape(rows, seq_n * col_width) for i in range(4)
    ]
    return (results[1], results[0], results[2], results[3])


def solution(mesh):
    in_specs = (
        P(("space", "seq"), None),
        P(("space", "seq"), None),
        P(("space", "seq"), None),
        P(("space", "seq"), None),
        P(),
        P("space", None),
        P("space", None),
    )
    out_specs = (
        P(("space", "seq"), None),
        P(("space", "seq"), None),
        P(("space", "seq"), None),
        P(("space", "seq"), None),
    )
    return jax.shard_map(shards, mesh=mesh, in_specs=in_specs, out_specs=out_specs, check_vma=False)
```

```python
import jax
import jax.numpy as jnp
from jax import lax
from jax.experimental import pallas as pl
from jax.experimental.pallas import tpu as pltpu
from jax.sharding import PartitionSpec as P

HEAD = 64
WIN = 64


MASKED_SCORE = -1e30


def padded(value, sides, width):
    for axis, dim in sides:
        count, length = (lax.axis_size(axis), value.shape[dim])
        up = [(i, (i + 1) % count) for i in range(count - 1)]
        down = [(j, i) for i, j in up]
        last = lax.slice_in_dim(value, length - width, length, axis=dim)
        first = lax.slice_in_dim(value, 0, width, axis=dim)
        before = lax.ppermute(last, axis, up)
        after = lax.ppermute(first, axis, down)
        value = jnp.concatenate([before, value, after], axis=dim)
    return value


def gather_rows(source, indices):
    return source.at[indices].get(mode="promise_in_bounds")


def to_windows(query_part, key_part, value_part, members):
    query_win = gather_rows(query_part, members)
    kv_win = gather_rows(jnp.concatenate([key_part, value_part], axis=1), members)
    return (query_win, kv_win)


def border_rows(source, border):
    return jnp.concatenate([source[:border], source[source.shape[0] - border :]], axis=0)


def extend_windows(kv_win, received, border):
    return jnp.concatenate([received[:border], kv_win, received[3 * border :]], axis=0)


def window_keys(block_id, per_block, border, neighbours):
    start_row = block_id * per_block
    own_rows = border + start_row + jnp.arange(per_block, dtype=jnp.int32)
    near_rows = lax.dynamic_slice_in_dim(neighbours, start_row, per_block, 0)
    return jnp.concatenate([own_rows[:, None], near_rows], axis=1)


def block_attention(query_blk, key_index, kv_ext, length_ext, head_count):
    block_n = query_blk.shape[0]
    col_width = query_blk.shape[-1]
    head_size = col_width // head_count
    key_rows = gather_rows(kv_ext, key_index).reshape(block_n, -1, 2 * col_width)
    key_length = gather_rows(length_ext, key_index)
    key_alive = (jnp.arange(WIN, dtype=jnp.int32)[None, None, :] < key_length[:, :, None]).reshape(
        block_n, -1
    )
    query_heads = query_blk.reshape(block_n, WIN, head_count, head_size)
    key_heads = key_rows[:, :, :col_width].reshape(block_n, -1, head_count, head_size)
    value_heads = key_rows[:, :, col_width:].reshape(block_n, -1, head_count, head_size)
    score_scale = head_size ** (-0.5)
    scores = (
        jnp.einsum("wqhd,wkhd->whqk", query_heads, key_heads, preferred_element_type=jnp.float32)
        * score_scale
    )
    scores = jnp.where(key_alive[:, None, None, :], scores, MASKED_SCORE)
    row_max = jnp.max(scores, axis=-1, keepdims=True)
    exp_scores = jnp.exp(scores - row_max)
    attn_probs = exp_scores / jnp.sum(exp_scores, axis=-1, keepdims=True)
    return (attn_probs, query_heads, key_heads, value_heads, score_scale)


def attention_kernel(idx_ref, len_ref, win_ref, kv_ref, out_ref, dkv_ref, rim_ref):
    windows_n = win_ref.shape[0]
    lanes = kv_ref.shape[-1]
    width = lanes // 2
    nb = idx_ref.shape[0] // windows_n
    keys = nb * WIN
    scale = HEAD ** (-0.5)
    dkv_ref[...] = jnp.zeros(dkv_ref.shape, dkv_ref.dtype)
    col = lax.broadcasted_iota(jnp.int32, (1, keys), 1)
    col_block = col // WIN
    col_slot = col % WIN
    lane = lax.broadcasted_iota(jnp.int32, (1, lanes), 1)
    first_half = lane < width
    slot_row = lax.broadcasted_iota(jnp.int32, (WIN, 1), 0)
    nt = (((1,), (1,)), ((), ()))
    tn = (((0,), (0,)), ((), ()))

    def body(w, carry):
        ids = [idx_ref[w * nb + j] for j in range(nb)]
        qg = win_ref[w, :, :lanes]
        zero = jnp.zeros_like(qg)
        q_pad = jnp.where(first_half, qg, zero)
        g_live = jnp.logical_and(jnp.logical_not(first_half), slot_row < len_ref[ids[0]])
        g_pad = jnp.where(g_live, qg, zero)
        qg_blocks = jnp.concatenate([q_pad, g_pad], axis=0)
        kv_all = jnp.concatenate([kv_ref[i] for i in ids], axis=0)
        limit = jnp.zeros((1, keys), jnp.int32)
        for j in range(nb):
            limit = jnp.where(col_block == j, len_ref[ids[j]], limit)
        alive = col_slot < limit
        both = lax.dot_general(qg_blocks, kv_all, nt, preferred_element_type=jnp.float32)
        scores = both[:WIN] * scale
        grad_probs = both[WIN:]
        scores = jnp.where(alive, scores, MASKED_SCORE)
        row_max = jnp.max(scores, axis=-1, keepdims=True)
        exp_scores = jnp.exp(scores - row_max)
        probs = exp_scores / jnp.sum(exp_scores, axis=-1, keepdims=True)
        weights = probs.astype(jnp.bfloat16)
        out_full = jnp.dot(weights, kv_all, preferred_element_type=jnp.float32).astype(jnp.bfloat16)
        delta = jnp.sum(
            g_pad.astype(jnp.float32) * out_full.astype(jnp.float32), axis=-1, keepdims=True
        )
        grad_scores = (probs * (grad_probs - delta) * scale).astype(jnp.bfloat16)
        dq_full = jnp.dot(grad_scores, kv_all, preferred_element_type=jnp.float32).astype(jnp.bfloat16)
        out_ref[w] = jnp.where(first_half, dq_full, out_full)
        score_blocks = jnp.concatenate([grad_scores, weights], axis=0)
        grad_kv = lax.dot_general(score_blocks, qg_blocks, tn, preferred_element_type=jnp.float32)
        for j in range(nb):
            dkv_ref[ids[j]] += grad_kv[j * WIN : (j + 1) * WIN]
        return carry

    lax.fori_loop(0, windows_n, body, 0, unroll=32)
    ext_n = dkv_ref.shape[0]
    border = rim_ref.shape[0] // 2
    rim_ref[:border] = dkv_ref[:border].astype(rim_ref.dtype)
    rim_ref[border:] = dkv_ref[ext_n - border :].astype(rim_ref.dtype)


def window_attention(key_index, length_ext, win_all, kv_ext):
    windows_n = win_all.shape[0]
    lanes = kv_ext.shape[-1]
    ext_n = kv_ext.shape[0]
    keys = (key_index.shape[0] // windows_n) * WIN
    flops = 2 * windows_n * WIN * keys * lanes * 6
    vmem = pl.BlockSpec(memory_space=pltpu.VMEM)
    smem = pl.BlockSpec(memory_space=pltpu.SMEM)
    return pl.pallas_call(
        attention_kernel,
        out_shape=(
            jax.ShapeDtypeStruct((windows_n, WIN, lanes), jnp.bfloat16),
            jax.ShapeDtypeStruct((ext_n, WIN, lanes), jnp.float32),
            jax.ShapeDtypeStruct((ext_n - windows_n, WIN, lanes), jnp.bfloat16),
        ),
        in_specs=[smem, smem, vmem, vmem],
        out_specs=(vmem, vmem, vmem),
        compiler_params=pltpu.CompilerParams(vmem_limit_bytes=48 * 1024 * 1024),
        cost_estimate=pl.CostEstimate(
            flops=flops, transcendentals=windows_n * WIN * keys, bytes_accessed=8 * 1024 * 1024
        ),
    )(key_index, length_ext, win_all, kv_ext)


def shards(query_feats, key_feats, value_feats, grad_output, lengths, members, neighbours):
    group_idx = lax.axis_index("space")
    groups = lax.axis_size("space")
    windows_n = members.shape[0]
    border = windows_n // 6
    per_block = 8
    block_count = windows_n // per_block
    col_width = query_feats.shape[1] // lax.axis_size("seq")
    head_count = col_width // HEAD
    own_length = lax.dynamic_index_in_dim(lengths, group_idx, 0, keepdims=False)
    before_length = lax.dynamic_index_in_dim(
        lengths, jnp.maximum(group_idx - 1, 0), 0, keepdims=False
    )
    after_length = lax.dynamic_index_in_dim(
        lengths, jnp.minimum(group_idx + 1, groups - 1), 0, keepdims=False
    )
    length_ext = jnp.concatenate(
        [
            jnp.where(group_idx > 0, before_length[windows_n - border :], 0),
            own_length,
            jnp.where(group_idx < groups - 1, after_length[:border], 0),
        ]
    )
    slot_alive = jnp.arange(WIN, dtype=jnp.int32)[None, :] < own_length[:, None]
    rows = query_feats.shape[0]
    seq_n = lax.axis_size("seq")
    stacked = jnp.stack(
        [
            jnp.transpose(part.reshape(rows, seq_n, col_width), (1, 0, 2))
            for part in (query_feats, grad_output, key_feats, value_feats)
        ],
        axis=2,
    ).reshape(seq_n, rows, 4 * col_width)
    heads_all = lax.all_to_all(stacked, "seq", split_axis=0, concat_axis=0, tiled=True)
    voxel_count = seq_n * rows
    table = heads_all.reshape(voxel_count, 4 * col_width)
    flat_slots = jnp.where(slot_alive, members, voxel_count).reshape(-1)
    slot_of = (
        jnp.zeros((voxel_count,), jnp.int32)
        .at[flat_slots]
        .set(jnp.arange(windows_n * WIN, dtype=jnp.int32), mode="drop")
    )

    table, slot_of = lax.optimization_barrier((table, slot_of))

    def to_voxels(slot_vals):
        return gather_rows(slot_vals.reshape(windows_n * WIN, -1), slot_of)

    win_all = gather_rows(table, members)
    kv_win = win_all[..., 2 * col_width :]
    received = padded(border_rows(kv_win, border), (("space", 0),), border)
    kv_ext = extend_windows(kv_win, received, border)

    key_index = jnp.concatenate(
        [border + jnp.arange(windows_n, dtype=jnp.int32)[:, None], neighbours], axis=1
    ).reshape(-1)
    dq_out, grad_ext, rim_grads = window_attention(key_index, length_ext, win_all, kv_ext)
    received_grads = padded(rim_grads, (("space", 0),), border).astype(jnp.float32)
    own_grads = grad_ext[border : border + windows_n]
    own_grads = own_grads.at[:border].add(received_grads[:border])
    own_grads = own_grads.at[windows_n - border :].add(received_grads[3 * border :])
    slot_vals = jnp.concatenate(
        [dq_out, own_grads.astype(jnp.bfloat16)], axis=-1
    )
    vox = to_voxels(slot_vals).reshape(seq_n, rows, 4 * col_width)
    back = lax.all_to_all(vox, "seq", split_axis=0, concat_axis=0, tiled=True)
    back = back.reshape(seq_n, rows, 4, col_width)
    results = [
        jnp.transpose(back[:, :, i], (1, 0, 2)).reshape(rows, seq_n * col_width) for i in range(4)
    ]
    return (results[1], results[0], results[2], results[3])


def solution(mesh):
    in_specs = (
        P(("space", "seq"), None),
        P(("space", "seq"), None),
        P(("space", "seq"), None),
        P(("space", "seq"), None),
        P(),
        P("space", None),
        P("space", None),
    )
    out_specs = (
        P(("space", "seq"), None),
        P(("space", "seq"), None),
        P(("space", "seq"), None),
        P(("space", "seq"), None),
    )
    return jax.shard_map(shards, mesh=mesh, in_specs=in_specs, out_specs=out_specs, check_vma=False)
```
